32 devices in a mesh: gx: 16 (over z, y, core), gy: 2 (over x).
Axes of the slice: x: 2, y: 2, z: 4, core: 2. Of those that a mesh axis runs over, the one named last changes fastest.
Arguments:
- eigen_vecs: bfloat16 [2, 3, 4, 64, 32, 512], P(None, None, None, 'gx', 'gy'), may hold values from -6 to 6
- gauge_links: float32 [2, 2, 3, 3, 4, 64, 32], P(None, None, None, None, None, 'gx', 'gy'), may hold values from -4 to 4
- directions: int32 [4], replicated, may hold values from 0 to 3, each once
- spin_map: int32 [4], replicated, may hold values from 0 to 3, each once
- perambulator: bfloat16 [2, 2048, 2048], P(None, ('gx', 'gy')), may hold values from -0.125 to 0.125
Outputs:
- elementals: float32 [4, 2, 512, 512], P(None, None, 'gx')
- contracted: bfloat16 [4, 2, 2048, 2048], P(None, None, ('gx', 'gy'))
The draws below stay inside these ranges and needn't reach their ends.
Inputs may be any that keep to these rules, and one draw needn't show every extreme that they name: `directions`: a permutation of the four hops: 0 and 1 are forward hops along x and y, 2 and 3 backward hops along x and y. `spin_map`: a permutation of the four spins.
All inputs are finite; a program needn't handle non-finite values.
Results may differ from the reference program's by a relative error of at most 0.0058.
Values may be sent and summed in bfloat16 or wider, within the bound.
No kernel may reach another device: no remote copies, remote signals or barrier semaphores. Data moves between devices by JAX's collectives and lax.ppermute only.
A program may use at most 128 MiB of HBM per device.

```python
import math
import jax
import jax.numpy as jnp
from jax import lax

NEV = 512
NDISP = 4
NZ = 4
NX = 64
NY = 32
PERAM = 2048


def level_of(rng, extent, pieces, low, top_value):
    def one(position, shards_of):
        draws = jax.random.uniform(jax.random.fold_in(jax.random.fold_in(rng, 6), position), (shards_of,), jnp.float32, low / len(pieces), top_value / len(pieces))
        return jnp.repeat(jnp.exp(draws), extent[position] // shards_of).reshape((-1,) + (1,) * (len(extent) - position - 1))

    loudness = one(*pieces[0])
    for cut in pieces[1:]:
        loudness = loudness * one(*cut)
    return loudness


def bell_draw(stream_key, dims, spread, most, split=(), kind=jnp.bfloat16):
    factor_of = level_of(stream_key, dims, split, -0.22, 0.18) if split else 1.0
    result = jax.random.normal(stream_key, dims, jnp.float32) * spread * factor_of
    return jnp.minimum(jnp.maximum(result, -most), most).astype(kind)


def setup_inputs(seed: int = 0) -> dict:
    key_list = jax.random.split(jax.random.key(seed), 6)
    return {
        "eigen_vecs": bell_draw(key_list[0], (2, 3, NZ, NX, NY, NEV), 1.0, 6.0, ((3, 16), (4, 2))),
        "gauge_links": bell_draw(key_list[1], (2, 2, 3, 3, NZ, NX, NY), 0.577, 4.0, ((5, 16), (6, 2)), jnp.float32),
        "directions": jax.random.permutation(key_list[2], 4).astype(jnp.int32),
        "spin_map": jax.random.permutation(key_list[3], 4).astype(jnp.int32),
        "perambulator": bell_draw(key_list[4], (2, PERAM, PERAM), PERAM ** -0.5, 0.125, ((1, 32),)),
    }


def colour_apply(gauge_link, colour_field, dagger):
    values = colour_field.astype(jnp.float32)
    rows_re = []
    rows_im = []
    for row in range(3):
        acc_re = jnp.zeros(values.shape[2:], jnp.float32)
        acc_im = jnp.zeros(values.shape[2:], jnp.float32)
        for column in range(3):
            if dagger:
                coef_re = gauge_link[0, column, row][..., None]
                coef_im = -gauge_link[1, column, row][..., None]
            else:
                coef_re = gauge_link[0, row, column][..., None]
                coef_im = gauge_link[1, row, column][..., None]
            acc_re = acc_re + coef_re * values[0, column] - coef_im * values[1, column]
            acc_im = acc_im + coef_re * values[1, column] + coef_im * values[0, column]
        rows_re.append(acc_re)
        rows_im.append(acc_im)
    return jnp.stack([jnp.stack(rows_re, 0), jnp.stack(rows_im, 0)], 0)

def gram_term(field, displaced):
    count = field.shape[-1]
    left_re = field[0].reshape(-1, count)
    left_im = field[1].reshape(-1, count)
    right_re = displaced[0].reshape(-1, count)
    right_im = displaced[1].reshape(-1, count)
    real = jnp.dot(left_re.T, right_re, preferred_element_type=jnp.float32) + jnp.dot(left_im.T, right_im, preferred_element_type=jnp.float32)
    imag = jnp.dot(left_re.T, right_im, preferred_element_type=jnp.float32) - jnp.dot(left_im.T, right_re, preferred_element_type=jnp.float32)
    return jnp.stack([real, imag], 0)

def displaced_plane(eigen_vecs, gauge_links, plane, heading):
    after = (plane + 1) % NX
    before = (plane - 1 + NX) % NX
    field_here = lax.dynamic_index_in_dim(eigen_vecs, plane, 3, keepdims=False)
    links_here = lax.dynamic_index_in_dim(gauge_links, plane, 5, keepdims=False)

    def forward_x():
        field_after = lax.dynamic_index_in_dim(eigen_vecs, after, 3, keepdims=False)
        return colour_apply(links_here[0], field_after, False).astype(jnp.bfloat16)

    def forward_y():
        return colour_apply(links_here[1], jnp.roll(field_here, -1, axis=3), False).astype(jnp.bfloat16)

    def backward_x():
        field_before = lax.dynamic_index_in_dim(eigen_vecs, before, 3, keepdims=False)
        links_before = lax.dynamic_index_in_dim(gauge_links, before, 5, keepdims=False)
        return colour_apply(links_before[0], field_before, True).astype(jnp.bfloat16)

    def backward_y():
        source_here = colour_apply(links_here[1], field_here, True).astype(jnp.bfloat16)
        return jnp.roll(source_here, 1, axis=3)
    return (field_here, lax.switch(heading, [forward_x, forward_y, backward_x, backward_y]))

def reference(eigen_vecs, gauge_links, directions, spin_map, perambulator):
    norm_factor = 1.0 / math.sqrt(3.0 * NX * NY * NZ)
    planes = jnp.arange(NX, dtype=jnp.int32)
    results = []
    for disp_index in range(NDISP):
        heading = directions[disp_index]

        def advance(running, plane):
            field_here, displaced = displaced_plane(eigen_vecs, gauge_links, plane, heading)
            return (running + gram_term(field_here, displaced), None)
        running, unused_out = lax.scan(advance, jnp.zeros((2, NEV, NEV), jnp.float32), planes)
        results.append(running * norm_factor)
    elementals = jnp.stack(results, 0)
    rounded = elementals.astype(jnp.bfloat16)
    onehot = (spin_map[:, None] == jnp.arange(4, dtype=jnp.int32)[None, :]).astype(jnp.float32)
    blocks = perambulator.reshape(2, PERAM, 4, NEV).astype(jnp.float32)
    chosen = jnp.einsum('prtn,st->prsn', blocks, onehot).astype(jnp.bfloat16)
    lhs_block = jnp.concatenate([chosen[0], chosen[1]], axis=-1).reshape(PERAM * 4, 2 * NEV)
    outputs = []
    for disp_index in range(NDISP):
        part_re = rounded[disp_index, 0]
        part_im = rounded[disp_index, 1]
        rhs_block = jnp.concatenate([jnp.concatenate([part_re, part_im], 1), jnp.concatenate([-part_im, part_re], 1)], 0)
        product = jnp.dot(lhs_block, rhs_block, preferred_element_type=jnp.float32)
        product = product.reshape(PERAM, 4, 2, NEV).transpose(2, 0, 1, 3).reshape(2, PERAM, PERAM)
        outputs.append(product.astype(jnp.bfloat16))
    return (elementals, jnp.stack(outputs, 0))
```

```python
import math

import jax
import jax.numpy as jnp
from jax import lax
from jax.sharding import PartitionSpec as P

ALL = ("gx", "gy")
STREAMS = 3


def colour_apply(gauge_link, colour_field, dagger):
    values = colour_field.astype(jnp.float32)
    rows_re = []
    rows_im = []
    for row in range(3):
        acc_re = jnp.zeros(values.shape[2:], jnp.float32)
        acc_im = jnp.zeros(values.shape[2:], jnp.float32)
        for column in range(3):
            if dagger:
                coef_re = gauge_link[0, column, row][..., None]
                coef_im = -gauge_link[1, column, row][..., None]
            else:
                coef_re = gauge_link[0, row, column][..., None]
                coef_im = gauge_link[1, row, column][..., None]
            acc_re = acc_re + coef_re * values[0, column] - coef_im * values[1, column]
            acc_im = acc_im + coef_re * values[1, column] + coef_im * values[0, column]
        rows_re.append(acc_re)
        rows_im.append(acc_im)
    return jnp.stack([jnp.stack(rows_re, 0), jnp.stack(rows_im, 0)], 0)


def bit_orders(mesh):
    devs = list(mesh.devices.reshape(-1))
    count = len(devs)
    nbits = count.bit_length() - 1

    def dist(a, b):
        try:
            da, db = devs[a], devs[b]
            return sum(abs(p - q) for p, q in zip(da.coords, db.coords))
        except Exception:
            return 1

    near, core, far = [], [], []
    for b in range(nbits):
        d = max(dist(i, i ^ (1 << b)) for i in range(count))
        (core if d == 0 else near if d == 1 else far).append(b)
    orders = []
    for s in range(STREAMS):
        k = s % max(len(near), 1)
        orders.append(core + near[k:] + near[:k] + far)
    return nbits, orders


def xor_pairs(count, b):
    return [(i, i ^ (1 << b)) for i in range(count)]


def reduce_scatter(buf, bits, nbits, count):
    idx = lax.axis_index(ALL)
    for b in bits:
        ax = nbits - 1 - b
        mine = (idx >> b) & 1
        keep = lax.dynamic_slice_in_dim(buf, mine, 1, axis=ax)
        send = lax.dynamic_slice_in_dim(buf, 1 - mine, 1, axis=ax)
        buf = keep + lax.ppermute(send, ALL, xor_pairs(count, b))
    return buf


def all_gather(buf, bits, nbits, count):
    idx = lax.axis_index(ALL)
    for b in bits:
        ax = nbits - 1 - b
        mine = (idx >> b) & 1
        other = lax.ppermute(buf, ALL, xor_pairs(count, b))
        lo = jnp.where(mine == 0, buf, other)
        hi = jnp.where(mine == 0, other, buf)
        buf = jnp.concatenate([lo, hi], axis=ax)
    return buf


def column_splits(total, parts):
    unit = 128
    units = total // unit
    sizes = [units // parts + (1 if s < units % parts else 0) for s in range(parts)]
    edges = [0]
    for s in sizes:
        edges.append(edges[-1] + s * unit)
    edges[-1] = total
    return [(edges[s], edges[s + 1]) for s in range(parts) if edges[s + 1] > edges[s]]


def make_local(nbits, orders):
    def local(eigen_vecs, gauge_links, directions, spin_map, perambulator):
        nx = lax.axis_size("gx")
        ny = lax.axis_size("gy")
        count = nx * ny
        _, ncol, nz, lx, ly, nev = eigen_vecs.shape
        ndisp = directions.shape[0]
        norm_factor = 1.0 / math.sqrt(3.0 * nz * lx * ly * count)
        ev = eigen_vecs

        src_x = colour_apply(gauge_links[0], ev, True).astype(jnp.bfloat16)
        src_y = colour_apply(gauge_links[1], ev, True).astype(jnp.bfloat16)
        up_x = lax.ppermute(ev[:, :, :, 0:1], "gx", [(i, (i - 1) % nx) for i in range(nx)])
        dn_x = lax.ppermute(src_x[:, :, :, lx - 1:], "gx", [(i, (i + 1) % nx) for i in range(nx)])
        up_y = lax.ppermute(ev[:, :, :, :, 0:1], "gy", [(i, (i - 1) % ny) for i in range(ny)])
        dn_y = lax.ppermute(src_y[:, :, :, :, ly - 1:], "gy", [(i, (i + 1) % ny) for i in range(ny)])
        ahead_x = jnp.concatenate([ev[:, :, :, 1:], up_x], axis=3)
        ahead_y = jnp.concatenate([ev[:, :, :, :, 1:], up_y], axis=4)
        disp = [
            colour_apply(gauge_links[0], ahead_x, False).astype(jnp.bfloat16),
            colour_apply(gauge_links[1], ahead_y, False).astype(jnp.bfloat16),
            jnp.concatenate([dn_x, src_x[:, :, :, : lx - 1]], axis=3),
            jnp.concatenate([dn_y, src_y[:, :, :, :, : ly - 1]], axis=4),
        ]
        depth = 2 * ncol * nz * lx * ly
        left = ev.reshape(depth, nev)
        right = []
        for d in disp:
            right.append(d.reshape(depth, nev))
            right.append(jnp.concatenate([d[1], -d[0]], axis=0).reshape(depth, nev))
        right = jnp.stack(right, axis=1).reshape(depth, 2 * len(disp) * nev)
        width = right.shape[1]
        gram = lax.dot_general(
            left, right, (((0,), (0,)), ((), ())), preferred_element_type=jnp.float32
        )
        rows = nev // count
        own = []
        pieces = column_splits(width, len(orders))
        for (a, b), order in zip(pieces, orders):
            buf = gram[:, a:b].reshape([2] * nbits + [rows, b - a])
            own.append(reduce_scatter(buf, order, nbits, count).reshape(rows, b - a))
        own = jnp.concatenate(own, axis=1) * norm_factor
        own = jnp.take(own.reshape(rows, len(disp), 2, nev), directions, axis=1)
        own_flat = own.reshape(rows, ndisp * 2 * nev)

        gy_bits = [b for b in range(nbits) if (1 << b) < ny]
        grown = all_gather(
            own_flat.reshape([1] * nbits + [rows, ndisp * 2 * nev]), gy_bits, nbits, count
        )
        elem = grown.reshape(ny * rows, ndisp, 2, nev).transpose(1, 2, 0, 3)

        rounded = own_flat.astype(jnp.bfloat16)
        full = []
        for (a, b), order in zip(pieces, orders):
            buf = rounded[:, a:b].reshape([1] * nbits + [rows, b - a])
            full.append(all_gather(buf, list(reversed(order)), nbits, count).reshape(nev, b - a))
        full = jnp.concatenate(full, axis=1).reshape(nev, ndisp, 2, nev)
        lower = jnp.stack([-full[:, :, 1], full[:, :, 0]], axis=2)
        rhs = jnp.concatenate([full, lower], axis=0).reshape(2 * nev, ndisp * 2 * nev)

        prows = perambulator.shape[1]
        nspin = perambulator.shape[2] // nev
        blocks = perambulator.reshape(2, prows, nspin, nev)
        chosen = jnp.take(blocks, spin_map, axis=2)
        lhs = chosen.transpose(1, 2, 0, 3).reshape(prows * nspin, 2 * nev)
        product = jnp.dot(lhs, rhs, preferred_element_type=jnp.float32).astype(jnp.bfloat16)
        contracted = (
            product.reshape(prows, nspin, ndisp, 2, nev)
            .transpose(2, 3, 0, 1, 4)
            .reshape(ndisp, 2, prows, nspin * nev)
        )
        return (elem, contracted)

    return local


def solution(mesh):
    nbits, orders = bit_orders(mesh)
    in_specs = (
        P(None, None, None, "gx", "gy", None),
        P(None, None, None, None, None, "gx", "gy"),
        P(),
        P(),
        P(None, ("gx", "gy"), None),
    )
    out_specs = (P(None, None, "gx", None), P(None, None, ("gx", "gy"), None))
    return jax.shard_map(
        make_local(nbits, orders), mesh=mesh, in_specs=in_specs, out_specs=out_specs, check_vma=False
    )
```

```python
import math

import jax
import jax.numpy as jnp
from jax import lax
from jax.sharding import PartitionSpec as P

ALL = ("gx", "gy")
STREAMS = 3


def colour_apply(gauge_link, colour_field, dagger):
    values = colour_field.astype(jnp.float32)
    rows_re = []
    rows_im = []
    for row in range(3):
        acc_re = jnp.zeros(values.shape[2:], jnp.float32)
        acc_im = jnp.zeros(values.shape[2:], jnp.float32)
        for column in range(3):
            if dagger:
                coef_re = gauge_link[0, column, row][..., None]
                coef_im = -gauge_link[1, column, row][..., None]
            else:
                coef_re = gauge_link[0, row, column][..., None]
                coef_im = gauge_link[1, row, column][..., None]
            acc_re = acc_re + coef_re * values[0, column] - coef_im * values[1, column]
            acc_im = acc_im + coef_re * values[1, column] + coef_im * values[0, column]
        rows_re.append(acc_re)
        rows_im.append(acc_im)
    return jnp.stack([jnp.stack(rows_re, 0), jnp.stack(rows_im, 0)], 0)


def bit_orders(mesh):
    devs = list(mesh.devices.reshape(-1))
    count = len(devs)
    nbits = count.bit_length() - 1

    def dist(a, b):
        try:
            da, db = devs[a], devs[b]
            return sum(abs(p - q) for p, q in zip(da.coords, db.coords))
        except Exception:
            return 1

    near, core, far = [], [], []
    for b in range(nbits):
        d = max(dist(i, i ^ (1 << b)) for i in range(count))
        (core if d == 0 else near if d == 1 else far).append(b)
    orders = []
    for s in range(STREAMS):
        k = s % max(len(near), 1)
        orders.append(core + near[k:] + near[:k] + far)
    return nbits, orders


def xor_pairs(count, b):
    return [(i, i ^ (1 << b)) for i in range(count)]


def reduce_scatter(buf, bits, nbits, count, lead):
    idx = lax.axis_index(ALL)
    for b in bits:
        ax = lead + nbits - 1 - b
        mine = (idx >> b) & 1
        keep = lax.dynamic_slice_in_dim(buf, mine, 1, axis=ax)
        send = lax.dynamic_slice_in_dim(buf, 1 - mine, 1, axis=ax)
        buf = keep + lax.ppermute(send, ALL, xor_pairs(count, b))
    return buf


def all_gather(buf, bits, nbits, count, lead):
    idx = lax.axis_index(ALL)
    for b in bits:
        ax = lead + nbits - 1 - b
        mine = (idx >> b) & 1
        other = lax.ppermute(buf, ALL, xor_pairs(count, b))
        lo = jnp.where(mine == 0, buf, other)
        hi = jnp.where(mine == 0, other, buf)
        buf = jnp.concatenate([lo, hi], axis=ax)
    return buf


def make_local(nbits, orders):
    def local(eigen_vecs, gauge_links, directions, spin_map, perambulator):
        nx = lax.axis_size("gx")
        ny = lax.axis_size("gy")
        count = nx * ny
        _, ncol, nz, lx, ly, nev = eigen_vecs.shape
        norm_factor = 1.0 / math.sqrt(3.0 * nz * lx * ly * count)
        ev = eigen_vecs

        src_x = colour_apply(gauge_links[0], ev, True).astype(jnp.bfloat16)
        src_y = colour_apply(gauge_links[1], ev, True).astype(jnp.bfloat16)
        up_x = lax.ppermute(ev[:, :, :, 0:1], "gx", [(i, (i - 1) % nx) for i in range(nx)])
        dn_x = lax.ppermute(src_x[:, :, :, lx - 1:], "gx", [(i, (i + 1) % nx) for i in range(nx)])
        up_y = lax.ppermute(ev[:, :, :, :, 0:1], "gy", [(i, (i - 1) % ny) for i in range(ny)])
        dn_y = lax.ppermute(src_y[:, :, :, :, ly - 1:], "gy", [(i, (i + 1) % ny) for i in range(ny)])
        ahead_x = jnp.concatenate([ev[:, :, :, 1:], up_x], axis=3)
        ahead_y = jnp.concatenate([ev[:, :, :, :, 1:], up_y], axis=4)
        disp = [
            colour_apply(gauge_links[0], ahead_x, False).astype(jnp.bfloat16),
            colour_apply(gauge_links[1], ahead_y, False).astype(jnp.bfloat16),
            jnp.concatenate([dn_x, src_x[:, :, :, : lx - 1]], axis=3),
            jnp.concatenate([dn_y, src_y[:, :, :, :, : ly - 1]], axis=4),
        ]
        depth = ncol * nz * lx * ly
        flat = ev.reshape(2, depth, nev)
        swapped = jnp.concatenate([-flat[1], flat[0]], axis=0)
        left = jnp.concatenate([flat.reshape(2 * depth, nev), swapped], axis=1)
        rows = nev // count

        prows = perambulator.shape[1]
        nspin = perambulator.shape[2] // nev
        chosen = jnp.take(perambulator.reshape(2, prows, nspin, nev), spin_map, axis=2)
        p_re, p_im = chosen[0], chosen[1]
        lhs = jnp.stack(
            [jnp.concatenate([p_re, -p_im], -1), jnp.concatenate([p_im, p_re], -1)], 0
        ).reshape(2 * prows * nspin, 2 * nev)

        own = []
        products = []
        for d, field in enumerate(disp):
            order = orders[d % len(orders)]
            gram = lax.dot_general(
                left, field.reshape(2 * depth, nev), (((0,), (0,)), ((), ())),
                preferred_element_type=jnp.float32,
            )
            buf = gram.reshape([2] + [2] * nbits + [rows, nev])
            part = reduce_scatter(buf, order, nbits, count, 1).reshape(2, rows, nev)
            part = part * norm_factor
            own.append(part)
            blk = part.astype(jnp.bfloat16).reshape([2] + [1] * nbits + [rows, nev])
            rhs = all_gather(blk, list(reversed(order)), nbits, count, 1).reshape(2 * nev, nev)
            product = jnp.dot(lhs, rhs, preferred_element_type=jnp.float32)
            products.append(product.astype(jnp.bfloat16).reshape(2, prows, nspin * nev))
        own = jnp.take(jnp.stack(own, 0), directions, axis=0)
        ndisp = own.shape[0]
        gy_bits = [b for b in range(nbits) if (1 << b) < ny]
        grown = all_gather(
            own.reshape([ndisp, 2] + [1] * nbits + [rows, nev]), gy_bits, nbits, count, 2
        )
        elem = grown.reshape(ndisp, 2, ny * rows, nev)
        contracted = jnp.take(jnp.stack(products, 0), directions, axis=0)
        return (elem, contracted)

    return local


def solution(mesh):
    nbits, orders = bit_orders(mesh)
    in_specs = (
        P(None, None, None, "gx", "gy", None),
        P(None, None, None, None, None, "gx", "gy"),
        P(),
        P(),
        P(None, ("gx", "gy"), None),
    )
    out_specs = (P(None, None, "gx", None), P(None, None, ("gx", "gy"), None))
    return jax.shard_map(
        make_local(nbits, orders), mesh=mesh, in_specs=in_specs, out_specs=out_specs, check_vma=False
    )
```

```python
import math

import jax
import jax.numpy as jnp
from jax import lax
from jax.sharding import PartitionSpec as P

ALL = ("gx", "gy")
STREAMS = 3


def colour_apply(gauge_link, colour_field, dagger):
    values = colour_field.astype(jnp.float32)
    rows_re = []
    rows_im = []
    for row in range(3):
        acc_re = jnp.zeros(values.shape[2:], jnp.float32)
        acc_im = jnp.zeros(values.shape[2:], jnp.float32)
        for column in range(3):
            if dagger:
                coef_re = gauge_link[0, column, row][..., None]
                coef_im = -gauge_link[1, column, row][..., None]
            else:
                coef_re = gauge_link[0, row, column][..., None]
                coef_im = gauge_link[1, row, column][..., None]
            acc_re = acc_re + coef_re * values[0, column] - coef_im * values[1, column]
            acc_im = acc_im + coef_re * values[1, column] + coef_im * values[0, column]
        rows_re.append(acc_re)
        rows_im.append(acc_im)
    return jnp.stack([jnp.stack(rows_re, 0), jnp.stack(rows_im, 0)], 0)


def bit_orders(mesh):
    devs = list(mesh.devices.reshape(-1))
    count = len(devs)
    nbits = count.bit_length() - 1

    def dist(a, b):
        try:
            da, db = devs[a], devs[b]
            return sum(abs(p - q) for p, q in zip(da.coords, db.coords))
        except Exception:
            return 1

    near, core, far = [], [], []
    for b in range(nbits):
        d = max(dist(i, i ^ (1 << b)) for i in range(count))
        (core if d == 0 else near if d == 1 else far).append(b)
    orders = []
    for s in range(STREAMS):
        k = s % max(len(near), 1)
        orders.append(core + near[k:] + near[:k] + far)
    return nbits, orders


def xor_pairs(count, b):
    return [(i, i ^ (1 << b)) for i in range(count)]


def reduce_scatter(buf, bits, nbits, count, lead):
    idx = lax.axis_index(ALL)
    for b in bits:
        ax = lead + nbits - 1 - b
        mine = (idx >> b) & 1
        keep = lax.dynamic_slice_in_dim(buf, mine, 1, axis=ax)
        send = lax.dynamic_slice_in_dim(buf, 1 - mine, 1, axis=ax)
        buf = keep + lax.ppermute(send, ALL, xor_pairs(count, b))
    return buf


def all_gather(buf, bits, nbits, count, lead):
    idx = lax.axis_index(ALL)
    for b in bits:
        ax = lead + nbits - 1 - b
        mine = (idx >> b) & 1
        other = lax.ppermute(buf, ALL, xor_pairs(count, b))
        lo = jnp.where(mine == 0, buf, other)
        hi = jnp.where(mine == 0, other, buf)
        buf = jnp.concatenate([lo, hi], axis=ax)
    return buf


def make_local(nbits, orders):
    def local(eigen_vecs, gauge_links, directions, spin_map, perambulator):
        nx = lax.axis_size("gx")
        ny = lax.axis_size("gy")
        count = nx * ny
        _, ncol, nz, lx, ly, nev = eigen_vecs.shape
        norm_factor = 1.0 / math.sqrt(3.0 * nz * lx * ly * count)
        ev = eigen_vecs

        src_x = colour_apply(gauge_links[0], ev, True).astype(jnp.bfloat16)
        src_y = colour_apply(gauge_links[1], ev, True).astype(jnp.bfloat16)
        up_x = lax.ppermute(ev[:, :, :, 0:1], "gx", [(i, (i - 1) % nx) for i in range(nx)])
        dn_x = lax.ppermute(src_x[:, :, :, lx - 1:], "gx", [(i, (i + 1) % nx) for i in range(nx)])
        up_y = lax.ppermute(ev[:, :, :, :, 0:1], "gy", [(i, (i - 1) % ny) for i in range(ny)])
        dn_y = lax.ppermute(src_y[:, :, :, :, ly - 1:], "gy", [(i, (i + 1) % ny) for i in range(ny)])
        ahead_x = jnp.concatenate([ev[:, :, :, 1:], up_x], axis=3)
        ahead_y = jnp.concatenate([ev[:, :, :, :, 1:], up_y], axis=4)
        disp = [
            colour_apply(gauge_links[0], ahead_x, False).astype(jnp.bfloat16),
            colour_apply(gauge_links[1], ahead_y, False).astype(jnp.bfloat16),
            jnp.concatenate([dn_x, src_x[:, :, :, : lx - 1]], axis=3),
            jnp.concatenate([dn_y, src_y[:, :, :, :, : ly - 1]], axis=4),
        ]
        depth = ncol * nz * lx * ly
        turned = ev.reshape(2, depth, nev).transpose(0, 2, 1)
        left = jnp.concatenate(
            [
                jnp.concatenate([turned[0], turned[1]], axis=1),
                jnp.concatenate([-turned[1], turned[0]], axis=1),
            ],
            axis=0,
        )
        rows = nev // count

        prows = perambulator.shape[1]
        nspin = perambulator.shape[2] // nev
        p_re = perambulator[0].reshape(prows * nspin, nev)
        p_im = perambulator[1].reshape(prows * nspin, nev)
        lhs = jnp.stack(
            [jnp.concatenate([p_re, -p_im], -1), jnp.concatenate([p_im, p_re], -1)], 0
        ).reshape(2, prows, nspin, 2 * nev)
        lhs = jnp.take(lhs, spin_map, axis=2).reshape(2 * prows * nspin, 2 * nev)

        own = []
        products = []
        for d, field in enumerate(disp):
            order = orders[d % len(orders)]
            gram = jnp.dot(left, field.reshape(2 * depth, nev), preferred_element_type=jnp.float32)
            buf = gram.reshape([2] + [2] * nbits + [rows, nev])
            part = reduce_scatter(buf, order, nbits, count, 1).reshape(2, rows, nev)
            part = part * norm_factor
            own.append(part)
            blk = part.astype(jnp.bfloat16).reshape([2] + [1] * nbits + [rows, nev])
            rhs = all_gather(blk, list(reversed(order)), nbits, count, 1).reshape(2 * nev, nev)
            product = jnp.dot(lhs, rhs, preferred_element_type=jnp.float32)
            products.append(product.astype(jnp.bfloat16).reshape(2, prows, nspin * nev))
        own = jnp.take(jnp.stack(own, 0), directions, axis=0)
        ndisp = own.shape[0]
        gy_bits = [b for b in range(nbits) if (1 << b) < ny]
        grown = all_gather(
            own.reshape([ndisp, 2] + [1] * nbits + [rows, nev]), gy_bits, nbits, count, 2
        )
        elem = grown.reshape(ndisp, 2, ny * rows, nev)
        contracted = jnp.take(jnp.stack(products, 0), directions, axis=0)
        return (elem, contracted)

    return local


def solution(mesh):
    nbits, orders = bit_orders(mesh)
    in_specs = (
        P(None, None, None, "gx", "gy", None),
        P(None, None, None, None, None, "gx", "gy"),
        P(),
        P(),
        P(None, ("gx", "gy"), None),
    )
    out_specs = (P(None, None, "gx", None), P(None, None, ("gx", "gy"), None))
    return jax.shard_map(
        make_local(nbits, orders), mesh=mesh, in_specs=in_specs, out_specs=out_specs, check_vma=False
    )
```

```python
import math

import jax
import jax.numpy as jnp
from jax import lax
from jax.sharding import PartitionSpec as P

ALL = ("gx", "gy")
SPLITS = 2


def colour_apply(gauge_link, colour_field, dagger):
    values = colour_field.astype(jnp.float32)
    rows_re = []
    rows_im = []
    for row in range(3):
        acc_re = jnp.zeros(values.shape[2:], jnp.float32)
        acc_im = jnp.zeros(values.shape[2:], jnp.float32)
        for column in range(3):
            if dagger:
                coef_re = gauge_link[0, column, row][..., None]
                coef_im = -gauge_link[1, column, row][..., None]
            else:
                coef_re = gauge_link[0, row, column][..., None]
                coef_im = gauge_link[1, row, column][..., None]
            acc_re = acc_re + coef_re * values[0, column] - coef_im * values[1, column]
            acc_im = acc_im + coef_re * values[1, column] + coef_im * values[0, column]
        rows_re.append(acc_re)
        rows_im.append(acc_im)
    return jnp.stack([jnp.stack(rows_re, 0), jnp.stack(rows_im, 0)], 0)


def bit_orders(mesh):
    devs = list(mesh.devices.reshape(-1))
    count = len(devs)
    nbits = count.bit_length() - 1

    def dist(a, b):
        try:
            da, db = devs[a], devs[b]
            return sum(abs(p - q) for p, q in zip(da.coords, db.coords))
        except Exception:
            return 1

    near, core, far = [], [], []
    for b in range(nbits):
        d = max(dist(i, i ^ (1 << b)) for i in range(count))
        (core if d == 0 else near if d == 1 else far).append(b)
    turns = [near[k:] + near[:k] for k in range(len(near))]
    back = near[::-1]
    turns += [back[k:] + back[:k] for k in range(len(near)) if len(near) > 2]
    orders = [core + t + far for t in turns] or [core + far]
    return nbits, orders


def xor_pairs(count, b):
    return [(i, i ^ (1 << b)) for i in range(count)]


def reduce_scatter(buf, bits, nbits, count, lead):
    idx = lax.axis_index(ALL)
    for b in bits:
        ax = lead + nbits - 1 - b
        mine = (idx >> b) & 1
        keep = lax.dynamic_slice_in_dim(buf, mine, 1, axis=ax)
        send = lax.dynamic_slice_in_dim(buf, 1 - mine, 1, axis=ax)
        buf = keep + lax.ppermute(send, ALL, xor_pairs(count, b))
    return buf


def all_gather(buf, bits, nbits, count, lead):
    idx = lax.axis_index(ALL)
    for b in bits:
        ax = lead + nbits - 1 - b
        mine = (idx >> b) & 1
        other = lax.ppermute(buf, ALL, xor_pairs(count, b))
        lo = jnp.where(mine == 0, buf, other)
        hi = jnp.where(mine == 0, other, buf)
        buf = jnp.concatenate([lo, hi], axis=ax)
    return buf


def make_local(nbits, orders):
    def local(eigen_vecs, gauge_links, directions, spin_map, perambulator):
        nx = lax.axis_size("gx")
        ny = lax.axis_size("gy")
        count = nx * ny
        _, ncol, nz, lx, ly, nev = eigen_vecs.shape
        norm_factor = 1.0 / math.sqrt(3.0 * nz * lx * ly * count)
        ev = eigen_vecs

        src_x = colour_apply(gauge_links[0], ev, True).astype(jnp.bfloat16)
        src_y = colour_apply(gauge_links[1], ev, True).astype(jnp.bfloat16)
        up_x = lax.ppermute(ev[:, :, :, 0:1], "gx", [(i, (i - 1) % nx) for i in range(nx)])
        dn_x = lax.ppermute(src_x[:, :, :, lx - 1:], "gx", [(i, (i + 1) % nx) for i in range(nx)])
        up_y = lax.ppermute(ev[:, :, :, :, 0:1], "gy", [(i, (i - 1) % ny) for i in range(ny)])
        dn_y = lax.ppermute(src_y[:, :, :, :, ly - 1:], "gy", [(i, (i + 1) % ny) for i in range(ny)])
        ahead_x = jnp.concatenate([ev[:, :, :, 1:], up_x], axis=3)
        ahead_y = jnp.concatenate([ev[:, :, :, :, 1:], up_y], axis=4)
        disp = [
            colour_apply(gauge_links[0], ahead_x, False).astype(jnp.bfloat16),
            colour_apply(gauge_links[1], ahead_y, False).astype(jnp.bfloat16),
            jnp.concatenate([dn_x, src_x[:, :, :, : lx - 1]], axis=3),
            jnp.concatenate([dn_y, src_y[:, :, :, :, : ly - 1]], axis=4),
        ]
        depth = ncol * nz * lx * ly
        turned = ev.reshape(2, depth, nev).transpose(0, 2, 1)
        left = jnp.concatenate(
            [
                jnp.concatenate([turned[0], turned[1]], axis=1),
                jnp.concatenate([-turned[1], turned[0]], axis=1),
            ],
            axis=0,
        )
        rows = nev // count

        prows = perambulator.shape[1]
        nspin = perambulator.shape[2] // nev
        p_re = perambulator[0].reshape(prows * nspin, nev)
        p_im = perambulator[1].reshape(prows * nspin, nev)
        lhs = jnp.stack(
            [jnp.concatenate([p_re, -p_im], -1), jnp.concatenate([p_im, p_re], -1)], 0
        ).reshape(2, prows, nspin, 2 * nev)
        lhs = jnp.take(lhs, spin_map, axis=2, mode="clip").reshape(2 * prows * nspin, 2 * nev)

        own = []
        products = []
        width = nev // SPLITS
        for d, field in enumerate(disp):
            gram = jnp.dot(left, field.reshape(2 * depth, nev), preferred_element_type=jnp.float32)
            gram = gram.reshape([2] + [2] * nbits + [rows, nev])
            own_parts = []
            prod_parts = []
            for h in range(SPLITS):
                order = orders[(d * SPLITS + h) % len(orders)]
                buf = lax.slice_in_dim(gram, h * width, (h + 1) * width, axis=nbits + 2)
                part = reduce_scatter(buf, order, nbits, count, 1).reshape(2, rows, width)
                part = part * norm_factor
                own_parts.append(part)
                blk = part.astype(jnp.bfloat16).reshape([2] + [1] * nbits + [rows, width])
                rhs = all_gather(blk, list(reversed(order)), nbits, count, 1).reshape(2 * nev, width)
                product = jnp.dot(lhs, rhs, preferred_element_type=jnp.float32)
                prod_parts.append(product.astype(jnp.bfloat16).reshape(2, prows, nspin, width))
            own.append(jnp.concatenate(own_parts, axis=-1))
            products.append(jnp.concatenate(prod_parts, axis=-1).reshape(2, prows, nspin * nev))
        own = jnp.take(jnp.stack(own, 0), directions, axis=0, mode="clip")
        ndisp = own.shape[0]
        gy_bits = [b for b in range(nbits) if (1 << b) < ny]
        grown = all_gather(
            own.reshape([ndisp, 2] + [1] * nbits + [rows, nev]), gy_bits, nbits, count, 2
        )
        elem = grown.reshape(ndisp, 2, ny * rows, nev)
        contracted = jnp.take(jnp.stack(products, 0), directions, axis=0, mode="clip")
        return (elem, contracted)

    return local


def solution(mesh):
    nbits, orders = bit_orders(mesh)
    in_specs = (
        P(None, None, None, "gx", "gy", None),
        P(None, None, None, None, None, "gx", "gy"),
        P(),
        P(),
        P(None, ("gx", "gy"), None),
    )
    out_specs = (P(None, None, "gx", None), P(None, None, ("gx", "gy"), None))
    return jax.shard_map(
        make_local(nbits, orders), mesh=mesh, in_specs=in_specs, out_specs=out_specs, check_vma=False
    )
```

```python
import math

import jax
import jax.numpy as jnp
from jax import lax
from jax.sharding import PartitionSpec as P

ALL = ("gx", "gy")
STREAMS = 3


def colour_apply(gauge_link, colour_field, dagger):
    values = colour_field.astype(jnp.float32)
    rows_re = []
    rows_im = []
    for row in range(3):
        acc_re = jnp.zeros(values.shape[2:], jnp.float32)
        acc_im = jnp.zeros(values.shape[2:], jnp.float32)
        for column in range(3):
            if dagger:
                coef_re = gauge_link[0, column, row][..., None]
                coef_im = -gauge_link[1, column, row][..., None]
            else:
                coef_re = gauge_link[0, row, column][..., None]
                coef_im = gauge_link[1, row, column][..., None]
            acc_re = acc_re + coef_re * values[0, column] - coef_im * values[1, column]
            acc_im = acc_im + coef_re * values[1, column] + coef_im * values[0, column]
        rows_re.append(acc_re)
        rows_im.append(acc_im)
    return jnp.stack([jnp.stack(rows_re, 0), jnp.stack(rows_im, 0)], 0)


def bit_orders(mesh):
    devs = list(mesh.devices.reshape(-1))
    count = len(devs)
    nbits = count.bit_length() - 1

    def dist(a, b):
        try:
            da, db = devs[a], devs[b]
            return sum(abs(p - q) for p, q in zip(da.coords, db.coords))
        except Exception:
            return 1

    near, core, far = [], [], []
    for b in range(nbits):
        d = max(dist(i, i ^ (1 << b)) for i in range(count))
        (core if d == 0 else near if d == 1 else far).append(b)
    orders = []
    for s in range(STREAMS):
        k = s % max(len(near), 1)
        orders.append(core + near[k:] + near[:k] + far)
    return nbits, orders


def xor_pairs(count, b):
    return [(i, i ^ (1 << b)) for i in range(count)]


def reduce_scatter(buf, bits, nbits, count, lead):
    idx = lax.axis_index(ALL)
    for b in bits:
        ax = lead + nbits - 1 - b
        mine = (idx >> b) & 1
        keep = lax.dynamic_slice_in_dim(buf, mine, 1, axis=ax)
        send = lax.dynamic_slice_in_dim(buf, 1 - mine, 1, axis=ax)
        buf = keep + lax.ppermute(send, ALL, xor_pairs(count, b))
    return buf


def all_gather(buf, bits, nbits, count, lead):
    idx = lax.axis_index(ALL)
    for b in bits:
        ax = lead + nbits - 1 - b
        mine = (idx >> b) & 1
        other = lax.ppermute(buf, ALL, xor_pairs(count, b))
        lo = jnp.where(mine == 0, buf, other)
        hi = jnp.where(mine == 0, other, buf)
        buf = jnp.concatenate([lo, hi], axis=ax)
    return buf


def column_splits(total, parts):
    unit = 128
    units = total // unit
    sizes = [units // parts + (1 if s < units % parts else 0) for s in range(parts)]
    edges = [0]
    for s in sizes:
        edges.append(edges[-1] + s * unit)
    edges[-1] = total
    return [(edges[s], edges[s + 1]) for s in range(parts) if edges[s + 1] > edges[s]]


def make_local(nbits, orders):
    def local(eigen_vecs, gauge_links, directions, spin_map, perambulator):
        nx = lax.axis_size("gx")
        ny = lax.axis_size("gy")
        count = nx * ny
        _, ncol, nz, lx, ly, nev = eigen_vecs.shape
        norm_factor = 1.0 / math.sqrt(3.0 * nz * lx * ly * count)
        ev = eigen_vecs

        src_x = colour_apply(gauge_links[0], ev, True).astype(jnp.bfloat16)
        src_y = colour_apply(gauge_links[1], ev, True).astype(jnp.bfloat16)
        up_x = lax.ppermute(ev[:, :, :, 0:1], "gx", [(i, (i - 1) % nx) for i in range(nx)])
        dn_x = lax.ppermute(src_x[:, :, :, lx - 1:], "gx", [(i, (i + 1) % nx) for i in range(nx)])
        up_y = lax.ppermute(ev[:, :, :, :, 0:1], "gy", [(i, (i - 1) % ny) for i in range(ny)])
        dn_y = lax.ppermute(src_y[:, :, :, :, ly - 1:], "gy", [(i, (i + 1) % ny) for i in range(ny)])
        ahead_x = jnp.concatenate([ev[:, :, :, 1:], up_x], axis=3)
        ahead_y = jnp.concatenate([ev[:, :, :, :, 1:], up_y], axis=4)
        disp = [
            colour_apply(gauge_links[0], ahead_x, False).astype(jnp.bfloat16),
            colour_apply(gauge_links[1], ahead_y, False).astype(jnp.bfloat16),
            jnp.concatenate([dn_x, src_x[:, :, :, : lx - 1]], axis=3),
            jnp.concatenate([dn_y, src_y[:, :, :, :, : ly - 1]], axis=4),
        ]
        depth = ncol * nz * lx * ly
        turned = ev.reshape(2, depth, nev).transpose(0, 2, 1)
        left = jnp.concatenate(
            [
                jnp.concatenate([turned[0], turned[1]], axis=1),
                jnp.concatenate([-turned[1], turned[0]], axis=1),
            ],
            axis=0,
        )
        rows = nev // count

        prows = perambulator.shape[1]
        nspin = perambulator.shape[2] // nev
        p_re = perambulator[0].reshape(prows * nspin, nev)
        p_im = perambulator[1].reshape(prows * nspin, nev)
        lhs = jnp.stack(
            [jnp.concatenate([p_re, -p_im], -1), jnp.concatenate([p_im, p_re], -1)], 0
        ).reshape(2 * prows * nspin, 2 * nev)

        ndisp = len(disp)
        fields = jnp.stack([d.reshape(2 * depth, nev) for d in disp], axis=1)
        gram = jnp.dot(left, fields.reshape(2 * depth, ndisp * nev), preferred_element_type=jnp.float32)
        gram = gram.reshape([2] + [2] * nbits + [rows, ndisp * nev])
        own = []
        products = []
        for (a, b), order in zip(column_splits(ndisp * nev, len(orders)), orders):
            buf = lax.slice_in_dim(gram, a, b, axis=nbits + 2)
            part = reduce_scatter(buf, order, nbits, count, 1).reshape(2, rows, b - a)
            part = part * norm_factor
            own.append(part)
            blk = part.astype(jnp.bfloat16).reshape([2] + [1] * nbits + [rows, b - a])
            rhs = all_gather(blk, list(reversed(order)), nbits, count, 1).reshape(2 * nev, b - a)
            products.append(jnp.dot(lhs, rhs, preferred_element_type=jnp.float32).astype(jnp.bfloat16))
        own = jnp.concatenate(own, axis=-1).reshape(2, rows, ndisp, nev)
        own = jnp.take(own, directions, axis=2, mode="clip").transpose(2, 0, 1, 3)
        gy_bits = [b for b in range(nbits) if (1 << b) < ny]
        grown = all_gather(
            own.reshape([ndisp, 2] + [1] * nbits + [rows, nev]), gy_bits, nbits, count, 2
        )
        elem = grown.reshape(ndisp, 2, ny * rows, nev)
        product = jnp.concatenate(products, axis=-1).reshape(2, prows, nspin, ndisp, nev)
        product = jnp.take(product, spin_map, axis=2, mode="clip")
        product = jnp.take(product, directions, axis=3, mode="clip")
        contracted = product.transpose(3, 0, 1, 2, 4).reshape(ndisp, 2, prows, nspin * nev)
        return (elem, contracted)

    return local


def solution(mesh):
    nbits, orders = bit_orders(mesh)
    in_specs = (
        P(None, None, None, "gx", "gy", None),
        P(None, None, None, None, None, "gx", "gy"),
        P(),
        P(),
        P(None, ("gx", "gy"), None),
    )
    out_specs = (P(None, None, "gx", None), P(None, None, ("gx", "gy"), None))
    return jax.shard_map(
        make_local(nbits, orders), mesh=mesh, in_specs=in_specs, out_specs=out_specs, check_vma=False
    )
```

```python
import math

import jax
import jax.numpy as jnp
from jax import lax
from jax.sharding import PartitionSpec as P

ALL = ("gx", "gy")
STREAMS = 3


def colour_apply(gauge_link, colour_field, dagger):
    values = colour_field.astype(jnp.float32)
    rows_re = []
    rows_im = []
    for row in range(3):
        acc_re = jnp.zeros(values.shape[2:], jnp.float32)
        acc_im = jnp.zeros(values.shape[2:], jnp.float32)
        for column in range(3):
            if dagger:
                coef_re = gauge_link[0, column, row][..., None]
                coef_im = -gauge_link[1, column, row][..., None]
            else:
                coef_re = gauge_link[0, row, column][..., None]
                coef_im = gauge_link[1, row, column][..., None]
            acc_re = acc_re + coef_re * values[0, column] - coef_im * values[1, column]
            acc_im = acc_im + coef_re * values[1, column] + coef_im * values[0, column]
        rows_re.append(acc_re)
        rows_im.append(acc_im)
    return jnp.stack([jnp.stack(rows_re, 0), jnp.stack(rows_im, 0)], 0)


def bit_orders(mesh):
    devs = list(mesh.devices.reshape(-1))
    count = len(devs)
    nbits = count.bit_length() - 1

    def dist(a, b):
        try:
            da, db = devs[a], devs[b]
            return sum(abs(p - q) for p, q in zip(da.coords, db.coords))
        except Exception:
            return 1

    near, core, far = [], [], []
    for b in range(nbits):
        d = max(dist(i, i ^ (1 << b)) for i in range(count))
        (core if d == 0 else near if d == 1 else far).append(b)
    orders = []
    for s in range(STREAMS):
        k = s % max(len(near), 1)
        orders.append(core + near[k:] + near[:k] + far)
    return nbits, orders


def xor_pairs(count, b):
    return [(i, i ^ (1 << b)) for i in range(count)]


def reduce_scatter(buf, bits, nbits, count, lead):
    idx = lax.axis_index(ALL)
    for b in bits:
        ax = lead + nbits - 1 - b
        mine = (idx >> b) & 1
        keep = lax.dynamic_slice_in_dim(buf, mine, 1, axis=ax)
        send = lax.dynamic_slice_in_dim(buf, 1 - mine, 1, axis=ax)
        buf = keep + lax.ppermute(send, ALL, xor_pairs(count, b))
    return buf


def all_gather(buf, bits, nbits, count, lead):
    idx = lax.axis_index(ALL)
    for b in bits:
        ax = lead + nbits - 1 - b
        mine = (idx >> b) & 1
        other = lax.ppermute(buf, ALL, xor_pairs(count, b))
        lo = jnp.where(mine == 0, buf, other)
        hi = jnp.where(mine == 0, other, buf)
        buf = jnp.concatenate([lo, hi], axis=ax)
    return buf


def make_local(nbits, orders):
    def local(eigen_vecs, gauge_links, directions, spin_map, perambulator):
        nx = lax.axis_size("gx")
        ny = lax.axis_size("gy")
        count = nx * ny
        _, ncol, nz, lx, ly, nev = eigen_vecs.shape
        norm_factor = 1.0 / math.sqrt(3.0 * nz * lx * ly * count)
        ev = eigen_vecs

        src_x = colour_apply(gauge_links[0], ev, True).astype(jnp.bfloat16)
        src_y = colour_apply(gauge_links[1], ev, True).astype(jnp.bfloat16)
        up_x = lax.ppermute(ev[:, :, :, 0:1], "gx", [(i, (i - 1) % nx) for i in range(nx)])
        dn_x = lax.ppermute(src_x[:, :, :, lx - 1:], "gx", [(i, (i + 1) % nx) for i in range(nx)])
        up_y = lax.ppermute(ev[:, :, :, :, 0:1], "gy", [(i, (i - 1) % ny) for i in range(ny)])
        dn_y = lax.ppermute(src_y[:, :, :, :, ly - 1:], "gy", [(i, (i + 1) % ny) for i in range(ny)])
        ahead_x = jnp.concatenate([ev[:, :, :, 1:], up_x], axis=3)
        ahead_y = jnp.concatenate([ev[:, :, :, :, 1:], up_y], axis=4)
        disp = [
            colour_apply(gauge_links[0], ahead_x, False).astype(jnp.bfloat16),
            colour_apply(gauge_links[1], ahead_y, False).astype(jnp.bfloat16),
            jnp.concatenate([dn_x, src_x[:, :, :, : lx - 1]], axis=3),
            jnp.concatenate([dn_y, src_y[:, :, :, :, : ly - 1]], axis=4),
        ]
        depth = ncol * nz * lx * ly
        turned = ev.reshape(2, depth, nev).transpose(0, 2, 1)
        left = jnp.concatenate(
            [
                jnp.concatenate([turned[0], turned[1]], axis=1),
                jnp.concatenate([-turned[1], turned[0]], axis=1),
            ],
            axis=0,
        )
        rows = nev // count

        prows = perambulator.shape[1]
        nspin = perambulator.shape[2] // nev

        def contraction_lhs(peram):
            chosen = jnp.stack(
                [lax.dynamic_slice_in_dim(peram, spin_map[u] * nev, nev, axis=2) for u in range(nspin)],
                axis=2,
            )
            p_re = chosen[0].reshape(prows * nspin, nev)
            p_im = chosen[1].reshape(prows * nspin, nev)
            return jnp.stack(
                [jnp.concatenate([p_re, -p_im], -1), jnp.concatenate([p_im, p_re], -1)], 0
            ).reshape(2 * prows * nspin, 2 * nev)

        lhs = None
        own = []
        products = []
        for d, field in enumerate(disp):
            order = orders[d % len(orders)]
            gram = jnp.dot(left, field.reshape(2 * depth, nev), preferred_element_type=jnp.float32)
            buf = gram.reshape([2] + [2] * nbits + [rows, nev])
            part = reduce_scatter(buf, order, nbits, count, 1).reshape(2, rows, nev)
            part = part * norm_factor
            own.append(part)
            if lhs is None:
                peram, _ = lax.optimization_barrier((perambulator, part))
                lhs = contraction_lhs(peram)
            blk = part.astype(jnp.bfloat16).reshape([2] + [1] * nbits + [rows, nev])
            rhs = all_gather(blk, list(reversed(order)), nbits, count, 1).reshape(2 * nev, nev)
            product = jnp.dot(lhs, rhs, preferred_element_type=jnp.float32)
            products.append(product.astype(jnp.bfloat16).reshape(2, prows, nspin * nev))
        own = jnp.take(jnp.stack(own, 0), directions, axis=0, mode="clip")
        ndisp = own.shape[0]
        gy_bits = [b for b in range(nbits) if (1 << b) < ny]
        grown = all_gather(
            own.reshape([ndisp, 2] + [1] * nbits + [rows, nev]), gy_bits, nbits, count, 2
        )
        elem = grown.reshape(ndisp, 2, ny * rows, nev)
        contracted = jnp.take(jnp.stack(products, 0), directions, axis=0, mode="clip")
        return (elem, contracted)

    return local


def solution(mesh):
    nbits, orders = bit_orders(mesh)
    in_specs = (
        P(None, None, None, "gx", "gy", None),
        P(None, None, None, None, None, "gx", "gy"),
        P(),
        P(),
        P(None, ("gx", "gy"), None),
    )
    out_specs = (P(None, None, "gx", None), P(None, None, ("gx", "gy"), None))
    return jax.shard_map(
        make_local(nbits, orders), mesh=mesh, in_specs=in_specs, out_specs=out_specs, check_vma=False
    )
```

```python
import math

import jax
import jax.numpy as jnp
from jax import lax
from jax.sharding import PartitionSpec as P

ALL = ("gx", "gy")
STREAMS = 3


def colour_apply(gauge_link, colour_field, dagger):
    values = colour_field.astype(jnp.float32)
    rows_re = []
    rows_im = []
    for row in range(3):
        acc_re = jnp.zeros(values.shape[2:], jnp.float32)
        acc_im = jnp.zeros(values.shape[2:], jnp.float32)
        for column in range(3):
            if dagger:
                coef_re = gauge_link[0, column, row][..., None]
                coef_im = -gauge_link[1, column, row][..., None]
            else:
                coef_re = gauge_link[0, row, column][..., None]
                coef_im = gauge_link[1, row, column][..., None]
            acc_re = acc_re + coef_re * values[0, column] - coef_im * values[1, column]
            acc_im = acc_im + coef_re * values[1, column] + coef_im * values[0, column]
        rows_re.append(acc_re)
        rows_im.append(acc_im)
    return jnp.stack([jnp.stack(rows_re, 0), jnp.stack(rows_im, 0)], 0)


def bit_orders(mesh):
    devs = list(mesh.devices.reshape(-1))
    count = len(devs)
    nbits = count.bit_length() - 1

    def dist(a, b):
        try:
            da, db = devs[a], devs[b]
            return sum(abs(p - q) for p, q in zip(da.coords, db.coords))
        except Exception:
            return 1

    near, core, far = [], [], []
    for b in range(nbits):
        d = max(dist(i, i ^ (1 << b)) for i in range(count))
        (core if d == 0 else near if d == 1 else far).append(b)
    orders = []
    for s in range(STREAMS):
        k = s % max(len(near), 1)
        orders.append(core + near[k:] + near[:k] + far)
    return nbits, orders


def xor_pairs(count, b):
    return [(i, i ^ (1 << b)) for i in range(count)]


def reduce_scatter(buf, bits, nbits, count, lead):
    idx = lax.axis_index(ALL)
    for b in bits:
        ax = lead + nbits - 1 - b
        mine = (idx >> b) & 1
        keep = lax.dynamic_slice_in_dim(buf, mine, 1, axis=ax)
        send = lax.dynamic_slice_in_dim(buf, 1 - mine, 1, axis=ax)
        buf = keep + lax.ppermute(send, ALL, xor_pairs(count, b))
    return buf


def all_gather(buf, bits, nbits, count, lead):
    idx = lax.axis_index(ALL)
    for b in bits:
        ax = lead + nbits - 1 - b
        mine = (idx >> b) & 1
        other = lax.ppermute(buf, ALL, xor_pairs(count, b))
        lo = jnp.where(mine == 0, buf, other)
        hi = jnp.where(mine == 0, other, buf)
        buf = jnp.concatenate([lo, hi], axis=ax)
    return buf


def make_local(nbits, orders):
    def local(eigen_vecs, gauge_links, directions, spin_map, perambulator):
        nx = lax.axis_size("gx")
        ny = lax.axis_size("gy")
        count = nx * ny
        _, ncol, nz, lx, ly, nev = eigen_vecs.shape
        norm_factor = 1.0 / math.sqrt(3.0 * nz * lx * ly * count)
        ev = eigen_vecs

        src_x = colour_apply(gauge_links[0], ev, True).astype(jnp.bfloat16)
        src_y = colour_apply(gauge_links[1], ev, True).astype(jnp.bfloat16)
        up_x = lax.ppermute(ev[:, :, :, 0:1], "gx", [(i, (i - 1) % nx) for i in range(nx)])
        dn_x = lax.ppermute(src_x[:, :, :, lx - 1:], "gx", [(i, (i + 1) % nx) for i in range(nx)])
        up_y = lax.ppermute(ev[:, :, :, :, 0:1], "gy", [(i, (i - 1) % ny) for i in range(ny)])
        dn_y = lax.ppermute(src_y[:, :, :, :, ly - 1:], "gy", [(i, (i + 1) % ny) for i in range(ny)])
        ahead_x = jnp.concatenate([ev[:, :, :, 1:], up_x], axis=3)
        ahead_y = jnp.concatenate([ev[:, :, :, :, 1:], up_y], axis=4)
        disp = [
            colour_apply(gauge_links[0], ahead_x, False).astype(jnp.bfloat16),
            colour_apply(gauge_links[1], ahead_y, False).astype(jnp.bfloat16),
            jnp.concatenate([dn_x, src_x[:, :, :, : lx - 1]], axis=3),
            jnp.concatenate([dn_y, src_y[:, :, :, :, : ly - 1]], axis=4),
        ]
        depth = ncol * nz * lx * ly
        turned = ev.reshape(2, depth, nev).transpose(0, 2, 1)
        left = jnp.concatenate(
            [
                jnp.concatenate([turned[0], turned[1]], axis=1),
                jnp.concatenate([-turned[1], turned[0]], axis=1),
            ],
            axis=0,
        )
        rows = nev // count

        prows = perambulator.shape[1]
        nspin = perambulator.shape[2] // nev
        p_re = perambulator[0].reshape(prows * nspin, nev)
        p_im = perambulator[1].reshape(prows * nspin, nev)
        lhs = jnp.stack(
            [jnp.concatenate([p_re, -p_im], -1), jnp.concatenate([p_im, p_re], -1)], 0
        ).reshape(2, prows, nspin, 2 * nev)
        lhs = jnp.take(lhs, spin_map, axis=2, mode="clip").reshape(2 * prows * nspin, 2 * nev)

        own = [None] * len(disp)
        products = [None] * len(disp)
        groups = {}
        for d in range(len(disp)):
            groups.setdefault(d % len(orders), []).append(d)
        for key, members in groups.items():
            order = orders[key]
            grams = [
                jnp.dot(left, disp[d].reshape(2 * depth, nev), preferred_element_type=jnp.float32)
                for d in members
            ]
            buf = jnp.stack(grams, 0).reshape([len(members), 2] + [2] * nbits + [rows, nev])
            part = reduce_scatter(buf, order, nbits, count, 2).reshape(len(members), 2, rows, nev)
            part = part * norm_factor
            blk = part.astype(jnp.bfloat16).reshape([len(members), 2] + [1] * nbits + [rows, nev])
            rhs = all_gather(blk, list(reversed(order)), nbits, count, 2)
            rhs = rhs.reshape(len(members), 2 * nev, nev)
            for m, d in enumerate(members):
                own[d] = part[m]
                product = jnp.dot(lhs, rhs[m], preferred_element_type=jnp.float32)
                products[d] = product.astype(jnp.bfloat16).reshape(2, prows, nspin * nev)
        own = jnp.take(jnp.stack(own, 0), directions, axis=0, mode="clip")
        ndisp = own.shape[0]
        gy_bits = [b for b in range(nbits) if (1 << b) < ny]
        grown = all_gather(
            own.reshape([ndisp, 2] + [1] * nbits + [rows, nev]), gy_bits, nbits, count, 2
        )
        elem = grown.reshape(ndisp, 2, ny * rows, nev)
        contracted = jnp.take(jnp.stack(products, 0), directions, axis=0, mode="clip")
        return (elem, contracted)

    return local


def solution(mesh):
    nbits, orders = bit_orders(mesh)
    in_specs = (
        P(None, None, None, "gx", "gy", None),
        P(None, None, None, None, None, "gx", "gy"),
        P(),
        P(),
        P(None, ("gx", "gy"), None),
    )
    out_specs = (P(None, None, "gx", None), P(None, None, ("gx", "gy"), None))
    return jax.shard_map(
        make_local(nbits, orders), mesh=mesh, in_specs=in_specs, out_specs=out_specs, check_vma=False
    )
```

```python
import math

import jax
import jax.numpy as jnp
from jax import lax
from jax.sharding import PartitionSpec as P

ALL = ("gx", "gy")
STREAMS = 3


def colour_apply(gauge_link, colour_field, dagger):
    values = colour_field.astype(jnp.float32)
    rows_re = []
    rows_im = []
    for row in range(3):
        acc_re = jnp.zeros(values.shape[2:], jnp.float32)
        acc_im = jnp.zeros(values.shape[2:], jnp.float32)
        for column in range(3):
            if dagger:
                coef_re = gauge_link[0, column, row][..., None]
                coef_im = -gauge_link[1, column, row][..., None]
            else:
                coef_re = gauge_link[0, row, column][..., None]
                coef_im = gauge_link[1, row, column][..., None]
            acc_re = acc_re + coef_re * values[0, column] - coef_im * values[1, column]
            acc_im = acc_im + coef_re * values[1, column] + coef_im * values[0, column]
        rows_re.append(acc_re)
        rows_im.append(acc_im)
    return jnp.stack([jnp.stack(rows_re, 0), jnp.stack(rows_im, 0)], 0)


def bit_orders(mesh):
    devs = list(mesh.devices.reshape(-1))
    count = len(devs)
    nbits = count.bit_length() - 1

    def dist(a, b):
        try:
            da, db = devs[a], devs[b]
            return sum(abs(p - q) for p, q in zip(da.coords, db.coords))
        except Exception:
            return 1

    near, core, far = [], [], []
    for b in range(nbits):
        d = max(dist(i, i ^ (1 << b)) for i in range(count))
        (core if d == 0 else near if d == 1 else far).append(b)
    orders = []
    for s in range(STREAMS):
        k = s % max(len(near), 1)
        orders.append(core + near[k:] + near[:k] + far)
    return nbits, orders


def xor_pairs(count, b):
    return [(i, i ^ (1 << b)) for i in range(count)]


def reduce_scatter(buf, bits, nbits, count, lead):
    idx = lax.axis_index(ALL)
    for b in bits:
        ax = lead + nbits - 1 - b
        mine = (idx >> b) & 1
        keep = lax.dynamic_slice_in_dim(buf, mine, 1, axis=ax)
        send = lax.dynamic_slice_in_dim(buf, 1 - mine, 1, axis=ax)
        buf = keep + lax.ppermute(send, ALL, xor_pairs(count, b))
    return buf


def all_gather(buf, bits, nbits, count, lead):
    idx = lax.axis_index(ALL)
    for b in bits:
        ax = lead + nbits - 1 - b
        mine = (idx >> b) & 1
        other = lax.ppermute(buf, ALL, xor_pairs(count, b))
        lo = jnp.where(mine == 0, buf, other)
        hi = jnp.where(mine == 0, other, buf)
        buf = jnp.concatenate([lo, hi], axis=ax)
    return buf


def make_local(nbits, orders):
    def local(eigen_vecs, gauge_links, directions, spin_map, perambulator):
        nx = lax.axis_size("gx")
        ny = lax.axis_size("gy")
        count = nx * ny
        _, ncol, nz, lx, ly, nev = eigen_vecs.shape
        norm_factor = 1.0 / math.sqrt(3.0 * nz * lx * ly * count)
        ev = eigen_vecs

        src_x = colour_apply(gauge_links[0], ev, True).astype(jnp.bfloat16)
        src_y = colour_apply(gauge_links[1], ev, True).astype(jnp.bfloat16)
        up_x = lax.ppermute(ev[:, :, :, 0:1], "gx", [(i, (i - 1) % nx) for i in range(nx)])
        dn_x = lax.ppermute(src_x[:, :, :, lx - 1:], "gx", [(i, (i + 1) % nx) for i in range(nx)])
        up_y = lax.ppermute(ev[:, :, :, :, 0:1], "gy", [(i, (i - 1) % ny) for i in range(ny)])
        dn_y = lax.ppermute(src_y[:, :, :, :, ly - 1:], "gy", [(i, (i + 1) % ny) for i in range(ny)])
        ahead_x = jnp.concatenate([ev[:, :, :, 1:], up_x], axis=3)
        ahead_y = jnp.concatenate([ev[:, :, :, :, 1:], up_y], axis=4)
        disp = [
            colour_apply(gauge_links[0], ahead_x, False).astype(jnp.bfloat16),
            colour_apply(gauge_links[1], ahead_y, False).astype(jnp.bfloat16),
            jnp.concatenate([dn_x, src_x[:, :, :, : lx - 1]], axis=3),
            jnp.concatenate([dn_y, src_y[:, :, :, :, : ly - 1]], axis=4),
        ]
        depth = ncol * nz * lx * ly
        turned = ev.reshape(2, depth, nev).transpose(0, 2, 1)
        left = jnp.concatenate(
            [
                jnp.concatenate([turned[0], turned[1]], axis=1),
                jnp.concatenate([-turned[1], turned[0]], axis=1),
            ],
            axis=0,
        )
        rows = nev // count

        prows = perambulator.shape[1]
        nspin = perambulator.shape[2] // nev
        p_re = perambulator[0].reshape(prows * nspin, nev)
        p_im = perambulator[1].reshape(prows * nspin, nev)
        lhs = jnp.stack(
            [jnp.concatenate([p_re, -p_im], -1), jnp.concatenate([p_im, p_re], -1)], 0
        ).reshape(2, prows, nspin, 2 * nev)
        lhs = jnp.take(lhs, spin_map, axis=2, mode="clip").reshape(2 * prows * nspin, 2 * nev)

        own = []
        products = []
        for d, field in enumerate(disp):
            order = orders[d % len(orders)]
            gram = jnp.dot(left, field.reshape(2 * depth, nev), preferred_element_type=jnp.float32)
            buf = gram.reshape([2] + [2] * nbits + [rows, nev])
            part = reduce_scatter(buf, order, nbits, count, 1).reshape(2, rows, nev)
            part = part * norm_factor
            own.append(part)
            blk = part.astype(jnp.bfloat16).reshape([2] + [1] * nbits + [rows, nev])
            rhs = all_gather(blk, list(reversed(order)), nbits, count, 1).reshape(2 * nev, nev)
            product = jnp.dot(lhs, rhs, preferred_element_type=jnp.float32)
            products.append(product.astype(jnp.bfloat16).reshape(2, prows, nspin * nev))
        own = jnp.take(jnp.stack(own, 0), directions, axis=0, mode="clip")
        ndisp = own.shape[0]
        gy_bits = [b for b in range(nbits) if (1 << b) < ny]
        grown = all_gather(
            own.reshape([ndisp, 2] + [1] * nbits + [rows, nev]), gy_bits, nbits, count, 2
        )
        elem = grown.reshape(ndisp, 2, ny * rows, nev)
        contracted = jnp.take(jnp.stack(products, 0), directions, axis=0, mode="clip")
        return (elem, contracted)

    return local


def solution(mesh):
    nbits, orders = bit_orders(mesh)
    in_specs = (
        P(None, None, None, "gx", "gy", None),
        P(None, None, None, None, None, "gx", "gy"),
        P(),
        P(),
        P(None, ("gx", "gy"), None),
    )
    out_specs = (P(None, None, "gx", None), P(None, None, ("gx", "gy"), None))
    return jax.shard_map(
        make_local(nbits, orders), mesh=mesh, in_specs=in_specs, out_specs=out_specs, check_vma=False
    )
```

```python
import math

import jax
import jax.numpy as jnp
from jax import lax
from jax.sharding import PartitionSpec as P

ALL = ("gx", "gy")
STREAMS = 3


def colour_apply(gauge_link, colour_field, dagger):
    values = colour_field.astype(jnp.float32)
    rows_re = []
    rows_im = []
    for row in range(3):
        acc_re = jnp.zeros(values.shape[2:], jnp.float32)
        acc_im = jnp.zeros(values.shape[2:], jnp.float32)
        for column in range(3):
            if dagger:
                coef_re = gauge_link[0, column, row][..., None]
                coef_im = -gauge_link[1, column, row][..., None]
            else:
                coef_re = gauge_link[0, row, column][..., None]
                coef_im = gauge_link[1, row, column][..., None]
            acc_re = acc_re + coef_re * values[0, column] - coef_im * values[1, column]
            acc_im = acc_im + coef_re * values[1, column] + coef_im * values[0, column]
        rows_re.append(acc_re)
        rows_im.append(acc_im)
    return jnp.stack([jnp.stack(rows_re, 0), jnp.stack(rows_im, 0)], 0)


def bit_orders(mesh):
    devs = list(mesh.devices.reshape(-1))
    count = len(devs)
    nbits = count.bit_length() - 1

    def dist(a, b):
        try:
            da, db = devs[a], devs[b]
            return sum(abs(p - q) for p, q in zip(da.coords, db.coords))
        except Exception:
            return 1

    near, core, far = [], [], []
    for b in range(nbits):
        d = max(dist(i, i ^ (1 << b)) for i in range(count))
        (core if d == 0 else near if d == 1 else far).append(b)
    orders = []
    for s in range(STREAMS):
        k = s % max(len(near), 1)
        orders.append(core + near[k:] + near[:k] + far)
    return nbits, orders


def xor_pairs(count, b):
    return [(i, i ^ (1 << b)) for i in range(count)]


def reduce_scatter(buf, bits, nbits, count, lead):
    idx = lax.axis_index(ALL)
    for b in bits:
        ax = lead + nbits - 1 - b
        mine = (idx >> b) & 1
        keep = lax.dynamic_slice_in_dim(buf, mine, 1, axis=ax)
        send = lax.dynamic_slice_in_dim(buf, 1 - mine, 1, axis=ax)
        buf = keep + lax.ppermute(send, ALL, xor_pairs(count, b))
    return buf


def all_gather(buf, bits, nbits, count, lead):
    idx = lax.axis_index(ALL)
    for b in bits:
        ax = lead + nbits - 1 - b
        mine = (idx >> b) & 1
        other = lax.ppermute(buf, ALL, xor_pairs(count, b))
        lo = jnp.where(mine == 0, buf, other)
        hi = jnp.where(mine == 0, other, buf)
        buf = jnp.concatenate([lo, hi], axis=ax)
    return buf


def make_local(nbits, orders):
    def local(eigen_vecs, gauge_links, directions, spin_map, perambulator):
        nx = lax.axis_size("gx")
        ny = lax.axis_size("gy")
        count = nx * ny
        _, ncol, nz, lx, ly, nev = eigen_vecs.shape
        norm_factor = 1.0 / math.sqrt(3.0 * nz * lx * ly * count)
        ev = eigen_vecs

        src_x = colour_apply(gauge_links[0], ev, True).astype(jnp.bfloat16)
        src_y = colour_apply(gauge_links[1], ev, True).astype(jnp.bfloat16)
        up_x = lax.ppermute(ev[:, :, :, 0:1], "gx", [(i, (i - 1) % nx) for i in range(nx)])
        dn_x = lax.ppermute(src_x[:, :, :, lx - 1:], "gx", [(i, (i + 1) % nx) for i in range(nx)])
        up_y = lax.ppermute(ev[:, :, :, :, 0:1], "gy", [(i, (i - 1) % ny) for i in range(ny)])
        dn_y = lax.ppermute(src_y[:, :, :, :, ly - 1:], "gy", [(i, (i + 1) % ny) for i in range(ny)])
        ahead_x = jnp.concatenate([ev[:, :, :, 1:], up_x], axis=3)
        ahead_y = jnp.concatenate([ev[:, :, :, :, 1:], up_y], axis=4)
        disp = [
            colour_apply(gauge_links[0], ahead_x, False).astype(jnp.bfloat16),
            colour_apply(gauge_links[1], ahead_y, False).astype(jnp.bfloat16),
            jnp.concatenate([dn_x, src_x[:, :, :, : lx - 1]], axis=3),
            jnp.concatenate([dn_y, src_y[:, :, :, :, : ly - 1]], axis=4),
        ]
        depth = ncol * nz * lx * ly
        turned = ev.reshape(2, depth, nev).transpose(0, 2, 1)
        left = jnp.concatenate(
            [
                jnp.concatenate([turned[0], turned[1]], axis=1),
                jnp.concatenate([-turned[1], turned[0]], axis=1),
            ],
            axis=0,
        )
        rows = nev // count

        prows = perambulator.shape[1]
        nspin = perambulator.shape[2] // nev
        p_re = perambulator[0].reshape(prows * nspin, nev)
        p_im = perambulator[1].reshape(prows * nspin, nev)
        lhs = jnp.stack(
            [jnp.concatenate([p_re, -p_im], -1), jnp.concatenate([p_im, p_re], -1)], 0
        ).reshape(2, prows, nspin, 2 * nev)
        lhs = jnp.take(lhs, spin_map, axis=2, mode="clip").reshape(2 * prows * nspin, 2 * nev)

        own = []
        products = []
        for d, field in enumerate(disp):
            order = orders[d % len(orders)]
            gram = jnp.dot(left, field.reshape(2 * depth, nev), preferred_element_type=jnp.float32)
            buf = gram.reshape([2] + [2] * nbits + [rows, nev])
            part = reduce_scatter(buf, order, nbits, count, 1).reshape(2, rows, nev)
            part = part * norm_factor
            own.append(part)
            blk = part.astype(jnp.bfloat16).reshape([2] + [1] * nbits + [rows, nev])
            rhs = all_gather(blk, list(reversed(order)), nbits, count, 1).reshape(2 * nev, nev)
            product = jnp.dot(lhs, rhs, preferred_element_type=jnp.float32)
            products.append(product.astype(jnp.bfloat16).reshape(2, prows, nspin * nev))
        own = jnp.take(jnp.stack(own, 0), directions, axis=0, mode="clip")
        ndisp = own.shape[0]
        gy_bits = [b for b in range(nbits) if (1 << b) < ny]
        grown = all_gather(
            own.reshape([ndisp, 2] + [1] * nbits + [rows, nev]), gy_bits, nbits, count, 2
        )
        elem = grown.reshape(ndisp, 2, ny * rows, nev)
        slots = jnp.arange(ndisp, dtype=directions.dtype)
        contracted = jnp.zeros((ndisp,) + products[0].shape, products[0].dtype)
        for d, product in enumerate(products):
            slot = jnp.sum(jnp.where(directions == d, slots, 0))
            contracted = lax.dynamic_update_slice_in_dim(contracted, product[None], slot, axis=0)
        return (elem, contracted)

    return local


def solution(mesh):
    nbits, orders = bit_orders(mesh)
    in_specs = (
        P(None, None, None, "gx", "gy", None),
        P(None, None, None, None, None, "gx", "gy"),
        P(),
        P(),
        P(None, ("gx", "gy"), None),
    )
    out_specs = (P(None, None, "gx", None), P(None, None, ("gx", "gy"), None))
    return jax.shard_map(
        make_local(nbits, orders), mesh=mesh, in_specs=in_specs, out_specs=out_specs, check_vma=False
    )
```

```python
import math

import jax
import jax.numpy as jnp
from jax import lax
from jax.sharding import PartitionSpec as P

ALL = ("gx", "gy")
STREAMS = 3


def colour_apply(gauge_link, colour_field, dagger):
    values = colour_field.astype(jnp.float32)
    rows_re = []
    rows_im = []
    for row in range(3):
        acc_re = jnp.zeros(values.shape[2:], jnp.float32)
        acc_im = jnp.zeros(values.shape[2:], jnp.float32)
        for column in range(3):
            if dagger:
                coef_re = gauge_link[0, column, row][..., None]
                coef_im = -gauge_link[1, column, row][..., None]
            else:
                coef_re = gauge_link[0, row, column][..., None]
                coef_im = gauge_link[1, row, column][..., None]
            acc_re = acc_re + coef_re * values[0, column] - coef_im * values[1, column]
            acc_im = acc_im + coef_re * values[1, column] + coef_im * values[0, column]
        rows_re.append(acc_re)
        rows_im.append(acc_im)
    return jnp.stack([jnp.stack(rows_re, 0), jnp.stack(rows_im, 0)], 0)


def bit_orders(mesh):
    devs = list(mesh.devices.reshape(-1))
    count = len(devs)
    nbits = count.bit_length() - 1

    def dist(a, b):
        try:
            da, db = devs[a], devs[b]
            return sum(abs(p - q) for p, q in zip(da.coords, db.coords))
        except Exception:
            return 1

    near, core, far = [], [], []
    for b in range(nbits):
        d = max(dist(i, i ^ (1 << b)) for i in range(count))
        (core if d == 0 else near if d == 1 else far).append(b)
    orders = []
    for s in range(STREAMS):
        k = s % max(len(near), 1)
        orders.append(core + near[k:] + near[:k] + far)
    return nbits, orders


def xor_pairs(count, b):
    return [(i, i ^ (1 << b)) for i in range(count)]


def reduce_scatter(buf, bits, nbits, count, lead):
    idx = lax.axis_index(ALL)
    for b in bits:
        ax = lead + nbits - 1 - b
        mine = (idx >> b) & 1
        keep = lax.dynamic_slice_in_dim(buf, mine, 1, axis=ax)
        send = lax.dynamic_slice_in_dim(buf, 1 - mine, 1, axis=ax)
        buf = keep + lax.ppermute(send, ALL, xor_pairs(count, b))
    return buf


def all_gather(buf, bits, nbits, count, lead):
    idx = lax.axis_index(ALL)
    for b in bits:
        ax = lead + nbits - 1 - b
        mine = (idx >> b) & 1
        other = lax.ppermute(buf, ALL, xor_pairs(count, b))
        lo = jnp.where(mine == 0, buf, other)
        hi = jnp.where(mine == 0, other, buf)
        buf = jnp.concatenate([lo, hi], axis=ax)
    return buf


def make_local(nbits, orders):
    def local(eigen_vecs, gauge_links, directions, spin_map, perambulator):
        nx = lax.axis_size("gx")
        ny = lax.axis_size("gy")
        count = nx * ny
        _, ncol, nz, lx, ly, nev = eigen_vecs.shape
        norm_factor = 1.0 / math.sqrt(3.0 * nz * lx * ly * count)
        ev = eigen_vecs

        src_x = colour_apply(gauge_links[0], ev, True).astype(jnp.bfloat16)
        src_y = colour_apply(gauge_links[1], ev, True).astype(jnp.bfloat16)
        up_x = lax.ppermute(ev[:, :, :, 0:1], "gx", [(i, (i - 1) % nx) for i in range(nx)])
        dn_x = lax.ppermute(src_x[:, :, :, lx - 1:], "gx", [(i, (i + 1) % nx) for i in range(nx)])
        up_y = lax.ppermute(ev[:, :, :, :, 0:1], "gy", [(i, (i - 1) % ny) for i in range(ny)])
        dn_y = lax.ppermute(src_y[:, :, :, :, ly - 1:], "gy", [(i, (i + 1) % ny) for i in range(ny)])
        ahead_x = jnp.concatenate([ev[:, :, :, 1:], up_x], axis=3)
        ahead_y = jnp.concatenate([ev[:, :, :, :, 1:], up_y], axis=4)
        disp = [
            colour_apply(gauge_links[0], ahead_x, False).astype(jnp.bfloat16),
            colour_apply(gauge_links[1], ahead_y, False).astype(jnp.bfloat16),
            jnp.concatenate([dn_x, src_x[:, :, :, : lx - 1]], axis=3),
            jnp.concatenate([dn_y, src_y[:, :, :, :, : ly - 1]], axis=4),
        ]
        depth = ncol * nz * lx * ly
        flat = ev.reshape(2, depth, nev)
        unit = jnp.eye(nev, dtype=ev.dtype)
        turned = [
            lax.dot_general(
                unit, flat[c], (((1,), (1,)), ((), ())), preferred_element_type=jnp.float32
            ).astype(ev.dtype)
            for c in range(2)
        ]
        left = jnp.concatenate(
            [
                jnp.concatenate([turned[0], turned[1]], axis=1),
                jnp.concatenate([-turned[1], turned[0]], axis=1),
            ],
            axis=0,
        )
        rows = nev // count

        prows = perambulator.shape[1]
        nspin = perambulator.shape[2] // nev
        p_re = perambulator[0].reshape(prows * nspin, nev)
        p_im = perambulator[1].reshape(prows * nspin, nev)
        lhs = jnp.stack(
            [jnp.concatenate([p_re, -p_im], -1), jnp.concatenate([p_im, p_re], -1)], 0
        ).reshape(2, prows, nspin, 2 * nev)
        lhs = jnp.take(lhs, spin_map, axis=2, mode="clip").reshape(2 * prows * nspin, 2 * nev)

        own = []
        products = []
        for d, field in enumerate(disp):
            order = orders[d % len(orders)]
            gram = jnp.dot(left, field.reshape(2 * depth, nev), preferred_element_type=jnp.float32)
            buf = gram.reshape([2] + [2] * nbits + [rows, nev])
            part = reduce_scatter(buf, order, nbits, count, 1).reshape(2, rows, nev)
            part = part * norm_factor
            own.append(part)
            blk = part.astype(jnp.bfloat16).reshape([2] + [1] * nbits + [rows, nev])
            rhs = all_gather(blk, list(reversed(order)), nbits, count, 1).reshape(2 * nev, nev)
            product = jnp.dot(lhs, rhs, preferred_element_type=jnp.float32)
            products.append(product.astype(jnp.bfloat16).reshape(2, prows, nspin * nev))
        own = jnp.take(jnp.stack(own, 0), directions, axis=0, mode="clip")
        ndisp = own.shape[0]
        gy_bits = [b for b in range(nbits) if (1 << b) < ny]
        grown = all_gather(
            own.reshape([ndisp, 2] + [1] * nbits + [rows, nev]), gy_bits, nbits, count, 2
        )
        elem = grown.reshape(ndisp, 2, ny * rows, nev)
        contracted = jnp.take(jnp.stack(products, 0), directions, axis=0, mode="clip")
        return (elem, contracted)

    return local


def solution(mesh):
    nbits, orders = bit_orders(mesh)
    in_specs = (
        P(None, None, None, "gx", "gy", None),
        P(None, None, None, None, None, "gx", "gy"),
        P(),
        P(),
        P(None, ("gx", "gy"), None),
    )
    out_specs = (P(None, None, "gx", None), P(None, None, ("gx", "gy"), None))
    return jax.shard_map(
        make_local(nbits, orders), mesh=mesh, in_specs=in_specs, out_specs=out_specs, check_vma=False
    )
```

```python
import math

import jax
import jax.numpy as jnp
from jax import lax
from jax.sharding import PartitionSpec as P

ALL = ("gx", "gy")
STREAMS = 3


def colour_apply(gauge_link, colour_field, dagger):
    values = colour_field.astype(jnp.float32)
    rows_re = []
    rows_im = []
    for row in range(3):
        acc_re = jnp.zeros(values.shape[2:], jnp.float32)
        acc_im = jnp.zeros(values.shape[2:], jnp.float32)
        for column in range(3):
            if dagger:
                coef_re = gauge_link[0, column, row][..., None]
                coef_im = -gauge_link[1, column, row][..., None]
            else:
                coef_re = gauge_link[0, row, column][..., None]
                coef_im = gauge_link[1, row, column][..., None]
            acc_re = acc_re + coef_re * values[0, column] - coef_im * values[1, column]
            acc_im = acc_im + coef_re * values[1, column] + coef_im * values[0, column]
        rows_re.append(acc_re)
        rows_im.append(acc_im)
    return jnp.stack([jnp.stack(rows_re, 0), jnp.stack(rows_im, 0)], 0)


def bit_orders(mesh):
    devs = list(mesh.devices.reshape(-1))
    count = len(devs)
    nbits = count.bit_length() - 1

    def dist(a, b):
        try:
            da, db = devs[a], devs[b]
            return sum(abs(p - q) for p, q in zip(da.coords, db.coords))
        except Exception:
            return 1

    near, core, far = [], [], []
    for b in range(nbits):
        d = max(dist(i, i ^ (1 << b)) for i in range(count))
        (core if d == 0 else near if d == 1 else far).append(b)
    orders = []
    for s in range(STREAMS):
        k = s % max(len(near), 1)
        orders.append(core + near[k:] + near[:k] + far)
    return nbits, orders


def xor_pairs(count, b):
    return [(i, i ^ (1 << b)) for i in range(count)]


def reduce_scatter(buf, bits, nbits, count, lead):
    idx = lax.axis_index(ALL)
    for b in bits:
        ax = lead + nbits - 1 - b
        mine = (idx >> b) & 1
        keep = lax.dynamic_slice_in_dim(buf, mine, 1, axis=ax)
        send = lax.dynamic_slice_in_dim(buf, 1 - mine, 1, axis=ax)
        buf = keep + lax.ppermute(send, ALL, xor_pairs(count, b))
    return buf


def all_gather(buf, bits, nbits, count, lead):
    idx = lax.axis_index(ALL)
    for b in bits:
        ax = lead + nbits - 1 - b
        mine = (idx >> b) & 1
        other = lax.ppermute(buf, ALL, xor_pairs(count, b))
        lo = jnp.where(mine == 0, buf, other)
        hi = jnp.where(mine == 0, other, buf)
        buf = jnp.concatenate([lo, hi], axis=ax)
    return buf


def make_local(nbits, orders):
    def local(eigen_vecs, gauge_links, directions, spin_map, perambulator):
        nx = lax.axis_size("gx")
        ny = lax.axis_size("gy")
        count = nx * ny
        _, ncol, nz, lx, ly, nev = eigen_vecs.shape
        norm_factor = 1.0 / math.sqrt(3.0 * nz * lx * ly * count)
        ev = eigen_vecs

        src_x = colour_apply(gauge_links[0], ev, True).astype(jnp.bfloat16)
        src_y = colour_apply(gauge_links[1], ev, True).astype(jnp.bfloat16)
        up_x = lax.ppermute(ev[:, :, :, 0:1], "gx", [(i, (i - 1) % nx) for i in range(nx)])
        dn_x = lax.ppermute(src_x[:, :, :, lx - 1:], "gx", [(i, (i + 1) % nx) for i in range(nx)])
        up_y = lax.ppermute(ev[:, :, :, :, 0:1], "gy", [(i, (i - 1) % ny) for i in range(ny)])
        dn_y = lax.ppermute(src_y[:, :, :, :, ly - 1:], "gy", [(i, (i + 1) % ny) for i in range(ny)])
        ahead_x = jnp.concatenate([ev[:, :, :, 1:], up_x], axis=3)
        ahead_y = jnp.concatenate([ev[:, :, :, :, 1:], up_y], axis=4)
        disp = [
            colour_apply(gauge_links[0], ahead_x, False).astype(jnp.bfloat16),
            colour_apply(gauge_links[1], ahead_y, False).astype(jnp.bfloat16),
            jnp.concatenate([dn_x, src_x[:, :, :, : lx - 1]], axis=3),
            jnp.concatenate([dn_y, src_y[:, :, :, :, : ly - 1]], axis=4),
        ]
        depth = ncol * nz * lx * ly
        flat = ev.reshape(2, depth, nev)
        unit = jnp.eye(nev, dtype=ev.dtype)
        turned = [
            lax.dot_general(
                unit, flat[c], (((1,), (1,)), ((), ())), preferred_element_type=jnp.float32
            ).astype(ev.dtype)
            for c in range(2)
        ]
        left = jnp.concatenate(
            [
                jnp.concatenate([turned[0], turned[1]], axis=1),
                jnp.concatenate([-turned[1], turned[0]], axis=1),
            ],
            axis=0,
        )
        rows = nev // count

        prows = perambulator.shape[1]
        nspin = perambulator.shape[2] // nev
        onehot = (spin_map[:, None] == jnp.arange(nspin, dtype=spin_map.dtype)[None, :]).astype(
            perambulator.dtype
        )
        chosen = jnp.einsum(
            "prtn,st->prsn", perambulator.reshape(2, prows, nspin, nev), onehot,
            preferred_element_type=jnp.float32,
        ).astype(perambulator.dtype)
        p_re = chosen[0].reshape(prows * nspin, nev)
        p_im = chosen[1].reshape(prows * nspin, nev)
        lhs = jnp.stack(
            [jnp.concatenate([p_re, -p_im], -1), jnp.concatenate([p_im, p_re], -1)], 0
        ).reshape(2 * prows * nspin, 2 * nev)

        own = []
        products = []
        for d, field in enumerate(disp):
            order = orders[d % len(orders)]
            gram = jnp.dot(left, field.reshape(2 * depth, nev), preferred_element_type=jnp.float32)
            buf = gram.reshape([2] + [2] * nbits + [rows, nev])
            part = reduce_scatter(buf, order, nbits, count, 1).reshape(2, rows, nev)
            part = part * norm_factor
            own.append(part)
            blk = part.astype(jnp.bfloat16).reshape([2] + [1] * nbits + [rows, nev])
            rhs = all_gather(blk, list(reversed(order)), nbits, count, 1).reshape(2 * nev, nev)
            product = jnp.dot(lhs, rhs, preferred_element_type=jnp.float32)
            products.append(product.astype(jnp.bfloat16).reshape(2, prows, nspin * nev))
        own = jnp.take(jnp.stack(own, 0), directions, axis=0, mode="clip")
        ndisp = own.shape[0]
        gy_bits = [b for b in range(nbits) if (1 << b) < ny]
        grown = all_gather(
            own.reshape([ndisp, 2] + [1] * nbits + [rows, nev]), gy_bits, nbits, count, 2
        )
        elem = grown.reshape(ndisp, 2, ny * rows, nev)
        contracted = jnp.take(jnp.stack(products, 0), directions, axis=0, mode="clip")
        return (elem, contracted)

    return local


def solution(mesh):
    nbits, orders = bit_orders(mesh)
    in_specs = (
        P(None, None, None, "gx", "gy", None),
        P(None, None, None, None, None, "gx", "gy"),
        P(),
        P(),
        P(None, ("gx", "gy"), None),
    )
    out_specs = (P(None, None, "gx", None), P(None, None, ("gx", "gy"), None))
    return jax.shard_map(
        make_local(nbits, orders), mesh=mesh, in_specs=in_specs, out_specs=out_specs, check_vma=False
    )
```

```python
import math

import jax
import jax.numpy as jnp
from jax import lax
from jax.sharding import PartitionSpec as P

ALL = ("gx", "gy")
STREAMS = 3


def colour_apply(gauge_link, colour_field, dagger):
    values = colour_field.astype(jnp.float32)
    rows_re = []
    rows_im = []
    for row in range(3):
        acc_re = jnp.zeros(values.shape[2:], jnp.float32)
        acc_im = jnp.zeros(values.shape[2:], jnp.float32)
        for column in range(3):
            if dagger:
                coef_re = gauge_link[0, column, row][..., None]
                coef_im = -gauge_link[1, column, row][..., None]
            else:
                coef_re = gauge_link[0, row, column][..., None]
                coef_im = gauge_link[1, row, column][..., None]
            acc_re = acc_re + coef_re * values[0, column] - coef_im * values[1, column]
            acc_im = acc_im + coef_re * values[1, column] + coef_im * values[0, column]
        rows_re.append(acc_re)
        rows_im.append(acc_im)
    return jnp.stack([jnp.stack(rows_re, 0), jnp.stack(rows_im, 0)], 0)


def bit_orders(mesh):
    devs = list(mesh.devices.reshape(-1))
    count = len(devs)
    nbits = count.bit_length() - 1

    def dist(a, b):
        try:
            da, db = devs[a], devs[b]
            return sum(abs(p - q) for p, q in zip(da.coords, db.coords))
        except Exception:
            return 1

    near, core, far = [], [], []
    for b in range(nbits):
        d = max(dist(i, i ^ (1 << b)) for i in range(count))
        (core if d == 0 else near if d == 1 else far).append(b)
    orders = []
    for s in range(STREAMS):
        k = s % max(len(near), 1)
        orders.append(core + near[k:] + near[:k] + far)
    return nbits, orders


def xor_pairs(count, b):
    return [(i, i ^ (1 << b)) for i in range(count)]


def reduce_scatter(buf, bits, nbits, count, lead):
    idx = lax.axis_index(ALL)
    for b in bits:
        ax = lead + nbits - 1 - b
        mine = (idx >> b) & 1
        keep = lax.dynamic_slice_in_dim(buf, mine, 1, axis=ax)
        send = lax.dynamic_slice_in_dim(buf, 1 - mine, 1, axis=ax)
        buf = keep + lax.ppermute(send, ALL, xor_pairs(count, b))
    return buf


def all_gather(buf, bits, nbits, count, lead):
    idx = lax.axis_index(ALL)
    for b in bits:
        ax = lead + nbits - 1 - b
        mine = (idx >> b) & 1
        other = lax.ppermute(buf, ALL, xor_pairs(count, b))
        lo = jnp.where(mine == 0, buf, other)
        hi = jnp.where(mine == 0, other, buf)
        buf = jnp.concatenate([lo, hi], axis=ax)
    return buf


def make_local(nbits, orders):
    def local(eigen_vecs, gauge_links, directions, spin_map, perambulator):
        nx = lax.axis_size("gx")
        ny = lax.axis_size("gy")
        count = nx * ny
        _, ncol, nz, lx, ly, nev = eigen_vecs.shape
        norm_factor = 1.0 / math.sqrt(3.0 * nz * lx * ly * count)
        ev = eigen_vecs

        src_x = colour_apply(gauge_links[0], ev, True).astype(jnp.bfloat16)
        src_y = colour_apply(gauge_links[1], ev, True).astype(jnp.bfloat16)
        up_x = lax.ppermute(ev[:, :, :, 0:1], "gx", [(i, (i - 1) % nx) for i in range(nx)])
        dn_x = lax.ppermute(src_x[:, :, :, lx - 1:], "gx", [(i, (i + 1) % nx) for i in range(nx)])
        up_y = lax.ppermute(ev[:, :, :, :, 0:1], "gy", [(i, (i - 1) % ny) for i in range(ny)])
        dn_y = lax.ppermute(src_y[:, :, :, :, ly - 1:], "gy", [(i, (i + 1) % ny) for i in range(ny)])
        ahead_x = jnp.concatenate([ev[:, :, :, 1:], up_x], axis=3)
        ahead_y = jnp.concatenate([ev[:, :, :, :, 1:], up_y], axis=4)
        disp = [
            colour_apply(gauge_links[0], ahead_x, False).astype(jnp.bfloat16),
            colour_apply(gauge_links[1], ahead_y, False).astype(jnp.bfloat16),
            jnp.concatenate([dn_x, src_x[:, :, :, : lx - 1]], axis=3),
            jnp.concatenate([dn_y, src_y[:, :, :, :, : ly - 1]], axis=4),
        ]
        depth = ncol * nz * lx * ly
        flat = ev.reshape(2, depth, nev)
        unit = jnp.eye(nev, dtype=ev.dtype)
        turned = [
            lax.dot_general(
                unit, flat[c], (((1,), (1,)), ((), ())), preferred_element_type=jnp.float32
            ).astype(ev.dtype)
            for c in range(2)
        ]
        left = jnp.concatenate(
            [
                jnp.concatenate([turned[0], turned[1]], axis=1),
                jnp.concatenate([-turned[1], turned[0]], axis=1),
            ],
            axis=0,
        )
        rows = nev // count

        prows = perambulator.shape[1]
        nspin = perambulator.shape[2] // nev
        onehot = (spin_map[:, None] == jnp.arange(nspin, dtype=spin_map.dtype)[None, :]).astype(
            perambulator.dtype
        )
        chosen = jnp.einsum(
            "prtn,st->prsn", perambulator.reshape(2, prows, nspin, nev), onehot,
            preferred_element_type=jnp.float32,
        ).astype(perambulator.dtype)
        p_re = chosen[0].reshape(prows * nspin, nev)
        p_im = chosen[1].reshape(prows * nspin, nev)
        lhs = jnp.stack(
            [jnp.concatenate([p_re, -p_im], -1), jnp.concatenate([p_im, p_re], -1)], 0
        ).reshape(2 * prows * nspin, 2 * nev)

        own = []
        products = []
        for d, field in enumerate(disp):
            order = orders[d % len(orders)]
            gram = jnp.dot(left, field.reshape(2 * depth, nev), preferred_element_type=jnp.float32)
            buf = gram.reshape([2] + [2] * nbits + [rows, nev])
            part = reduce_scatter(buf, order, nbits, count, 1).reshape(2, rows, nev)
            part = part * norm_factor
            own.append(part)
            blk = part.astype(jnp.bfloat16).reshape([2] + [1] * nbits + [rows, nev])
            rhs = all_gather(blk, list(reversed(order)), nbits, count, 1).reshape(2 * nev, nev)
            product = jnp.dot(lhs, rhs, preferred_element_type=jnp.float32)
            products.append(product.astype(jnp.bfloat16).reshape(2, prows, nspin * nev))
        own = jnp.take(jnp.stack(own, 0), directions, axis=0, mode="clip")
        ndisp = own.shape[0]
        gy_bits = [b for b in range(nbits) if (1 << b) < ny]
        grown = all_gather(
            own.reshape([ndisp, 2] + [1] * nbits + [rows, nev]), gy_bits, nbits, count, 2
        )
        elem = grown.reshape(ndisp, 2, ny * rows, nev)
        pick = (directions[:, None] == jnp.arange(ndisp, dtype=directions.dtype)[None, :]).astype(
            products[0].dtype
        )
        contracted = jnp.einsum(
            "kd,dcrm->kcrm", pick, jnp.stack(products, 0), preferred_element_type=jnp.float32
        ).astype(products[0].dtype)
        return (elem, contracted)

    return local


def solution(mesh):
    nbits, orders = bit_orders(mesh)
    in_specs = (
        P(None, None, None, "gx", "gy", None),
        P(None, None, None, None, None, "gx", "gy"),
        P(),
        P(),
        P(None, ("gx", "gy"), None),
    )
    out_specs = (P(None, None, "gx", None), P(None, None, ("gx", "gy"), None))
    return jax.shard_map(
        make_local(nbits, orders), mesh=mesh, in_specs=in_specs, out_specs=out_specs, check_vma=False
    )
```

```python
import math

import jax
import jax.numpy as jnp
from jax import lax
from jax.sharding import PartitionSpec as P

ALL = ("gx", "gy")
STREAMS = 3


def colour_apply(gauge_link, colour_field, dagger):
    values = colour_field
    rows_re = []
    rows_im = []
    for row in range(3):
        acc_re = jnp.zeros(values.shape[2:], jnp.float32)
        acc_im = jnp.zeros(values.shape[2:], jnp.float32)
        for column in range(3):
            if dagger:
                coef_re = gauge_link[0, column, row][..., None]
                coef_im = -gauge_link[1, column, row][..., None]
            else:
                coef_re = gauge_link[0, row, column][..., None]
                coef_im = gauge_link[1, row, column][..., None]
            acc_re = acc_re + coef_re * values[0, column] - coef_im * values[1, column]
            acc_im = acc_im + coef_re * values[1, column] + coef_im * values[0, column]
        rows_re.append(acc_re)
        rows_im.append(acc_im)
    return jnp.stack([jnp.stack(rows_re, 0), jnp.stack(rows_im, 0)], 0)


def bit_orders(mesh):
    devs = list(mesh.devices.reshape(-1))
    count = len(devs)
    nbits = count.bit_length() - 1

    def dist(a, b):
        try:
            da, db = devs[a], devs[b]
            return sum(abs(p - q) for p, q in zip(da.coords, db.coords))
        except Exception:
            return 1

    near, core, far = [], [], []
    for b in range(nbits):
        d = max(dist(i, i ^ (1 << b)) for i in range(count))
        (core if d == 0 else near if d == 1 else far).append(b)
    orders = []
    for s in range(STREAMS):
        k = s % max(len(near), 1)
        orders.append(core + near[k:] + near[:k] + far)
    return nbits, orders


def xor_pairs(count, b):
    return [(i, i ^ (1 << b)) for i in range(count)]


def reduce_scatter(buf, bits, nbits, count, lead):
    idx = lax.axis_index(ALL)
    for b in bits:
        ax = lead + nbits - 1 - b
        mine = (idx >> b) & 1
        keep = lax.dynamic_slice_in_dim(buf, mine, 1, axis=ax)
        send = lax.dynamic_slice_in_dim(buf, 1 - mine, 1, axis=ax)
        buf = keep + lax.ppermute(send, ALL, xor_pairs(count, b))
    return buf


def all_gather(buf, bits, nbits, count, lead):
    idx = lax.axis_index(ALL)
    for b in bits:
        ax = lead + nbits - 1 - b
        mine = (idx >> b) & 1
        other = lax.ppermute(buf, ALL, xor_pairs(count, b))
        lo = jnp.where(mine == 0, buf, other)
        hi = jnp.where(mine == 0, other, buf)
        buf = jnp.concatenate([lo, hi], axis=ax)
    return buf


def make_local(nbits, orders):
    def local(eigen_vecs, gauge_links, directions, spin_map, perambulator):
        nx = lax.axis_size("gx")
        ny = lax.axis_size("gy")
        count = nx * ny
        _, ncol, nz, lx, ly, nev = eigen_vecs.shape
        norm_factor = 1.0 / math.sqrt(3.0 * nz * lx * ly * count)
        ev = eigen_vecs

        src_x = colour_apply(gauge_links[0], ev, True).astype(jnp.bfloat16)
        src_y = colour_apply(gauge_links[1], ev, True).astype(jnp.bfloat16)
        up_x = lax.ppermute(ev[:, :, :, 0:1], "gx", [(i, (i - 1) % nx) for i in range(nx)])
        dn_x = lax.ppermute(src_x[:, :, :, lx - 1:], "gx", [(i, (i + 1) % nx) for i in range(nx)])
        up_y = lax.ppermute(ev[:, :, :, :, 0:1], "gy", [(i, (i - 1) % ny) for i in range(ny)])
        dn_y = lax.ppermute(src_y[:, :, :, :, ly - 1:], "gy", [(i, (i + 1) % ny) for i in range(ny)])
        ahead_x = jnp.concatenate([ev[:, :, :, 1:], up_x], axis=3)
        ahead_y = jnp.concatenate([ev[:, :, :, :, 1:], up_y], axis=4)
        disp = [
            colour_apply(gauge_links[0], ahead_x, False).astype(jnp.bfloat16),
            colour_apply(gauge_links[1], ahead_y, False).astype(jnp.bfloat16),
            jnp.concatenate([dn_x, src_x[:, :, :, : lx - 1]], axis=3),
            jnp.concatenate([dn_y, src_y[:, :, :, :, : ly - 1]], axis=4),
        ]
        depth = ncol * nz * lx * ly
        flat = ev.reshape(2, depth, nev)
        unit = jnp.eye(nev, dtype=ev.dtype)
        turned = [
            lax.dot_general(
                unit, flat[c], (((1,), (1,)), ((), ())), preferred_element_type=jnp.float32
            ).astype(ev.dtype)
            for c in range(2)
        ]
        left = jnp.concatenate(
            [
                jnp.concatenate([turned[0], turned[1]], axis=1),
                jnp.concatenate([-turned[1], turned[0]], axis=1),
            ],
            axis=0,
        )
        rows = nev // count

        prows = perambulator.shape[1]
        nspin = perambulator.shape[2] // nev
        onehot = (spin_map[:, None] == jnp.arange(nspin, dtype=spin_map.dtype)[None, :]).astype(
            perambulator.dtype
        )
        chosen = jnp.einsum(
            "prtn,st->prsn", perambulator.reshape(2, prows, nspin, nev), onehot,
            preferred_element_type=jnp.float32,
        ).astype(perambulator.dtype)
        p_re = chosen[0].reshape(prows * nspin, nev)
        p_im = chosen[1].reshape(prows * nspin, nev)
        lhs = jnp.stack(
            [jnp.concatenate([p_re, -p_im], -1), jnp.concatenate([p_im, p_re], -1)], 0
        ).reshape(2 * prows * nspin, 2 * nev)

        own = []
        products = []
        for d, field in enumerate(disp):
            order = orders[d % len(orders)]
            gram = jnp.dot(left, field.reshape(2 * depth, nev), preferred_element_type=jnp.float32)
            buf = gram.reshape([2] + [2] * nbits + [rows, nev])
            part = reduce_scatter(buf, order, nbits, count, 1).reshape(2, rows, nev)
            part = part * norm_factor
            own.append(part)
            blk = part.astype(jnp.bfloat16).reshape([2] + [1] * nbits + [rows, nev])
            rhs = all_gather(blk, list(reversed(order)), nbits, count, 1).reshape(2 * nev, nev)
            product = jnp.dot(lhs, rhs, preferred_element_type=jnp.float32)
            products.append(product.astype(jnp.bfloat16).reshape(2, prows, nspin * nev))
        own = jnp.take(jnp.stack(own, 0), directions, axis=0, mode="clip")
        ndisp = own.shape[0]
        gy_bits = [b for b in range(nbits) if (1 << b) < ny]
        grown = all_gather(
            own.reshape([ndisp, 2] + [1] * nbits + [rows, nev]), gy_bits, nbits, count, 2
        )
        elem = grown.reshape(ndisp, 2, ny * rows, nev)
        contracted = jnp.take(jnp.stack(products, 0), directions, axis=0, mode="clip")
        return (elem, contracted)

    return local


def solution(mesh):
    nbits, orders = bit_orders(mesh)
    in_specs = (
        P(None, None, None, "gx", "gy", None),
        P(None, None, None, None, None, "gx", "gy"),
        P(),
        P(),
        P(None, ("gx", "gy"), None),
    )
    out_specs = (P(None, None, "gx", None), P(None, None, ("gx", "gy"), None))
    return jax.shard_map(
        make_local(nbits, orders), mesh=mesh, in_specs=in_specs, out_specs=out_specs, check_vma=False
    )
```

```python
import math

import jax
import jax.numpy as jnp
from jax import lax
from jax.sharding import PartitionSpec as P

ALL = ("gx", "gy")
STREAMS = 3


def colour_apply(gauge_link, colour_field, dagger):
    values = colour_field.astype(jnp.float32)
    rows_re = []
    rows_im = []
    for row in range(3):
        acc_re = jnp.zeros(values.shape[2:], jnp.float32)
        acc_im = jnp.zeros(values.shape[2:], jnp.float32)
        for column in range(3):
            if dagger:
                coef_re = gauge_link[0, column, row][..., None]
                coef_im = -gauge_link[1, column, row][..., None]
            else:
                coef_re = gauge_link[0, row, column][..., None]
                coef_im = gauge_link[1, row, column][..., None]
            acc_re = acc_re + coef_re * values[0, column] - coef_im * values[1, column]
            acc_im = acc_im + coef_re * values[1, column] + coef_im * values[0, column]
        rows_re.append(acc_re)
        rows_im.append(acc_im)
    return jnp.stack([jnp.stack(rows_re, 0), jnp.stack(rows_im, 0)], 0)


def bit_orders(mesh):
    devs = list(mesh.devices.reshape(-1))
    count = len(devs)
    nbits = count.bit_length() - 1

    def dist(a, b):
        try:
            da, db = devs[a], devs[b]
            return sum(abs(p - q) for p, q in zip(da.coords, db.coords))
        except Exception:
            return 1

    near, core, far = [], [], []
    for b in range(nbits):
        d = max(dist(i, i ^ (1 << b)) for i in range(count))
        (core if d == 0 else near if d == 1 else far).append(b)
    orders = []
    for s in range(STREAMS):
        k = s % max(len(near), 1)
        orders.append(core + near[k:] + near[:k] + far)
    return nbits, orders


def xor_pairs(count, b):
    return [(i, i ^ (1 << b)) for i in range(count)]


def reduce_scatter(buf, bits, nbits, count, lead):
    idx = lax.axis_index(ALL)
    for b in bits:
        ax = lead + nbits - 1 - b
        mine = (idx >> b) & 1
        keep = lax.dynamic_slice_in_dim(buf, mine, 1, axis=ax)
        send = lax.dynamic_slice_in_dim(buf, 1 - mine, 1, axis=ax)
        buf = keep + lax.ppermute(send, ALL, xor_pairs(count, b))
    return buf


def all_gather(buf, bits, nbits, count, lead):
    idx = lax.axis_index(ALL)
    for b in bits:
        ax = lead + nbits - 1 - b
        mine = (idx >> b) & 1
        other = lax.ppermute(buf, ALL, xor_pairs(count, b))
        buf = jnp.where(
            mine == 0,
            jnp.concatenate([buf, other], axis=ax),
            jnp.concatenate([other, buf], axis=ax),
        )
    return buf


def make_local(nbits, orders):
    def local(eigen_vecs, gauge_links, directions, spin_map, perambulator):
        nx = lax.axis_size("gx")
        ny = lax.axis_size("gy")
        count = nx * ny
        _, ncol, nz, lx, ly, nev = eigen_vecs.shape
        norm_factor = 1.0 / math.sqrt(3.0 * nz * lx * ly * count)
        ev = eigen_vecs

        src_x = colour_apply(gauge_links[0], ev, True).astype(jnp.bfloat16)
        src_y = colour_apply(gauge_links[1], ev, True).astype(jnp.bfloat16)
        up_x = lax.ppermute(ev[:, :, :, 0:1], "gx", [(i, (i - 1) % nx) for i in range(nx)])
        dn_x = lax.ppermute(src_x[:, :, :, lx - 1:], "gx", [(i, (i + 1) % nx) for i in range(nx)])
        up_y = lax.ppermute(ev[:, :, :, :, 0:1], "gy", [(i, (i - 1) % ny) for i in range(ny)])
        dn_y = lax.ppermute(src_y[:, :, :, :, ly - 1:], "gy", [(i, (i + 1) % ny) for i in range(ny)])
        ahead_x = jnp.concatenate([ev[:, :, :, 1:], up_x], axis=3)
        ahead_y = jnp.concatenate([ev[:, :, :, :, 1:], up_y], axis=4)
        disp = [
            colour_apply(gauge_links[0], ahead_x, False).astype(jnp.bfloat16),
            colour_apply(gauge_links[1], ahead_y, False).astype(jnp.bfloat16),
            jnp.concatenate([dn_x, src_x[:, :, :, : lx - 1]], axis=3),
            jnp.concatenate([dn_y, src_y[:, :, :, :, : ly - 1]], axis=4),
        ]
        depth = ncol * nz * lx * ly
        flat = ev.reshape(2, depth, nev)
        unit = jnp.eye(nev, dtype=ev.dtype)
        turned = [
            lax.dot_general(
                unit, flat[c], (((1,), (1,)), ((), ())), preferred_element_type=jnp.float32
            ).astype(ev.dtype)
            for c in range(2)
        ]
        left = jnp.concatenate(
            [
                jnp.concatenate([turned[0], turned[1]], axis=1),
                jnp.concatenate([-turned[1], turned[0]], axis=1),
            ],
            axis=0,
        )
        rows = nev // count

        prows = perambulator.shape[1]
        nspin = perambulator.shape[2] // nev
        onehot = (spin_map[:, None] == jnp.arange(nspin, dtype=spin_map.dtype)[None, :]).astype(
            perambulator.dtype
        )
        chosen = jnp.einsum(
            "prtn,st->prsn", perambulator.reshape(2, prows, nspin, nev), onehot,
            preferred_element_type=jnp.float32,
        ).astype(perambulator.dtype)
        p_re = chosen[0].reshape(prows * nspin, nev)
        p_im = chosen[1].reshape(prows * nspin, nev)
        lhs = jnp.stack(
            [jnp.concatenate([p_re, -p_im], -1), jnp.concatenate([p_im, p_re], -1)], 0
        ).reshape(2 * prows * nspin, 2 * nev)

        own = []
        products = []
        for d, field in enumerate(disp):
            order = orders[d % len(orders)]
            gram = jnp.dot(left, field.reshape(2 * depth, nev), preferred_element_type=jnp.float32)
            buf = gram.reshape([2] + [2] * nbits + [rows, nev])
            part = reduce_scatter(buf, order, nbits, count, 1).reshape(2, rows, nev)
            part = part * norm_factor
            own.append(part)
            blk = part.astype(jnp.bfloat16).reshape([2] + [1] * nbits + [rows, nev])
            rhs = all_gather(blk, list(reversed(order)), nbits, count, 1).reshape(2 * nev, nev)
            product = jnp.dot(lhs, rhs, preferred_element_type=jnp.float32)
            products.append(product.astype(jnp.bfloat16).reshape(2, prows, nspin * nev))
        own = jnp.take(jnp.stack(own, 0), directions, axis=0, mode="clip")
        ndisp = own.shape[0]
        gy_bits = [b for b in range(nbits) if (1 << b) < ny]
        grown = all_gather(
            own.reshape([ndisp, 2] + [1] * nbits + [rows, nev]), gy_bits, nbits, count, 2
        )
        elem = grown.reshape(ndisp, 2, ny * rows, nev)
        contracted = jnp.take(jnp.stack(products, 0), directions, axis=0, mode="clip")
        return (elem, contracted)

    return local


def solution(mesh):
    nbits, orders = bit_orders(mesh)
    in_specs = (
        P(None, None, None, "gx", "gy", None),
        P(None, None, None, None, None, "gx", "gy"),
        P(),
        P(),
        P(None, ("gx", "gy"), None),
    )
    out_specs = (P(None, None, "gx", None), P(None, None, ("gx", "gy"), None))
    return jax.shard_map(
        make_local(nbits, orders), mesh=mesh, in_specs=in_specs, out_specs=out_specs, check_vma=False
    )
```
